256 devices in a mesh: people: 2 (over x_hi), tm: 64 (over z, y, core), type: 2 (over x_lo).
Axes of the slice: x: 4 (x_hi: 2, x_lo: 2; x = x_hi * 2 + x_lo), y: 4, z: 8, core: 2. Of those that a mesh axis runs over, the one named last changes fastest.
Arguments:
- features: bfloat16 [3, 2, 16384], P(None, 'people', 'tm'), may hold values from -6 to 6
- wear: int32 [2, 16384], P('people', 'tm'), may hold values 0 or 1
- rec_start: int32 [2], P('people'), may hold values from 0 to 255
- rec_end: int32 [2], P('people'), may hold values from 16129 to 16384
- conv_first: bfloat16 [3, 3, 128], replicated, may hold values from -2 to 2
- conv_second: bfloat16 [3, 128, 128], replicated, may hold values from -0.3125 to 0.3125
- emit_weight: bfloat16 [128, 512], P(None, 'type'), may hold values from -0.5 to 0.5
- leave: float32 [8, 64], P('type'), may hold values from 0.002 to 0.5
- jump: float32 [8, 64, 64], P('type'), may hold values from -6 to 6
- init_logits: float32 [8, 64], P('type'), may hold values from -6 to 6
- type_prior: float32 [8], replicated, may hold values from -4 to 4
Outputs:
- loglik_rate: float32 [2, 8], P('people', 'type')
- type_post: float32 [2, 8], P('people', 'type')
- occupancy: float32 [8, 64], P('type')
- filtered: float32 [2, 16384, 8, 64], P('people', 'tm', 'type')
The draws below stay inside these ranges and needn't reach their ends.
All inputs are finite; a program needn't handle non-finite values. No bound on the sum of `wear` on one device may be relied on, other than what follows from the above.
Results may differ from the reference program's by a relative error of at most 0.0085.
Values may be sent and summed in bfloat16 or wider, within the bound.
No kernel may reach another device: no remote copies, remote signals or barrier semaphores. Data moves between devices by JAX's collectives and lax.ppermute only.
A program may use at most 64 MiB of HBM per device.

```python
import math
import jax
import jax.numpy as jnp
from jax import lax

S = 64
K = 8
C = 128
CIN = 3
EP_DEV = 256
PEOPLE = 2
NE = 16384


def touch_ends(values, stream_key, least, largest):
    shape = values.shape
    spot = [jax.random.randint(jax.random.fold_in(stream_key, axis), (), 0, shape[axis]) for axis in range(len(shape))]
    values = values.at[tuple(spot)].set(least)
    longest = shape.index(max(shape))
    spot[longest] = (spot[longest] + 1) % shape[longest]
    return values.at[tuple(spot)].set(largest)


def block_levels(stream_key, dims, split, smallest, largest):
    def one(position, shards_of):
        heights = jax.random.uniform(jax.random.fold_in(jax.random.fold_in(stream_key, 6), position), (shards_of,), jnp.float32, smallest / len(split), largest / len(split))
        return jnp.repeat(jnp.exp(heights), dims[position] // shards_of).reshape((-1,) + (1,) * (len(dims) - position - 1))

    level = one(*split[0])
    for cut in split[1:]:
        level = level * one(*cut)
    return level


def normal_values(own_key, dims, scale, limit, cuts=(), held_as=jnp.bfloat16):
    entries = scale * jax.random.normal(own_key, dims, jnp.float32)
    if cuts:
        entries = entries * block_levels(own_key, dims, cuts, -0.22, 0.18)
    return jnp.clip(entries, -limit, limit).astype(held_as)


def setup_inputs(seed: int = 0) -> dict:
    keys = jax.random.split(jax.random.key(seed), 12)
    return {
        "features": normal_values(keys[0], (CIN, PEOPLE, NE), 1.0, 6.0, ((1, 2), (2, 64))),
        "wear": touch_ends((jax.random.randint(keys[1], (PEOPLE, NE), 0, 5) < 4).astype(jnp.int32), jax.random.fold_in(keys[1], 1), 0, 1),
        "rec_start": jax.random.randint(keys[2], (PEOPLE,), 0, EP_DEV).astype(jnp.int32),
        "rec_end": jax.random.randint(keys[3], (PEOPLE,), NE - EP_DEV + 1, NE + 1).astype(jnp.int32),
        "conv_first": normal_values(keys[4], (3, CIN, C), (3 * CIN) ** -0.5, 2.0),
        "conv_second": normal_values(keys[5], (3, C, C), (3 * C) ** -0.5, 0.3125),
        "emit_weight": normal_values(keys[6], (C, K * S), C ** -0.5, 0.5, ((1, 2),)),
        "leave": jnp.clip(jnp.exp(math.log(0.5) - 5.521461 * jax.random.uniform(keys[7], (K, S), jnp.float32) ** block_levels(keys[7], (K, S), ((0, 2),), -0.2, 0.2)), 0.002, 0.5),
        "jump": normal_values(keys[8], (K, S, S), 1.0, 6.0, ((0, 2),), jnp.float32),
        "init_logits": normal_values(keys[9], (K, S), 1.0, 6.0, ((0, 2),), jnp.float32),
        "type_prior": normal_values(keys[10], (K,), 1.0, 4.0, (), jnp.float32),
    }


def conv_layer(signal, weights, dilation):
    length = signal.shape[1]
    padded = jnp.pad(signal, ((0, 0), (dilation, dilation), (0, 0)))
    total = jnp.zeros(signal.shape[:2] + (weights.shape[2],), jnp.float32)
    for tap in range(3):
        piece = padded[:, tap * dilation: tap * dilation + length, :]
        total = total + jnp.einsum('ptc,cd->ptd', piece.astype(jnp.float32), weights[tap].astype(jnp.float32))
    return total


def transitions(leave, jump):
    eye = jnp.eye(jump.shape[-1], dtype=jnp.float32)
    return (1.0 - leave)[..., None] * eye + leave[..., None] * jax.nn.softmax(jump, axis=-1)


def reference(features, wear, rec_start, rec_end, conv_first, conv_second, emit_weight, leave, jump, init_logits, type_prior):
    persons = features.shape[1]
    epochs = features.shape[2]
    kinds = jump.shape[0]
    states = jump.shape[-1]
    signal = jnp.transpose(features, (1, 2, 0))
    first = jax.nn.silu(conv_layer(signal, conv_first, 1)).astype(jnp.bfloat16)
    second = jax.nn.silu(conv_layer(first, conv_second, 4)).astype(jnp.bfloat16)
    logits = jnp.einsum('ptc,cm->ptm', second.astype(jnp.float32), emit_weight.astype(jnp.float32))
    probs = jnp.exp(jax.nn.log_softmax(logits.reshape(persons, epochs, kinds, states), axis=-1))
    steps_all = jnp.arange(epochs, dtype=jnp.int32)
    observed = (wear > 0) & (steps_all[None, :] >= rec_start[:, None]) & (steps_all[None, :] < rec_end[:, None])
    emis = jnp.where(observed[:, :, None, None], probs, jnp.float32(1.0))
    observed_f = observed.astype(jnp.float32)
    trans = transitions(leave, jump)
    start = jax.nn.softmax(init_logits, axis=-1)

    def advance(carry, inputs):
        alpha, loglik, occupied = carry
        emis_now, mask_now = inputs
        pred = jnp.einsum('pki,kij->pkj', alpha, trans, precision=lax.Precision.HIGHEST)
        unnorm = pred * emis_now
        total = jnp.sum(unnorm, axis=-1)
        alpha = unnorm / total[..., None]
        loglik = loglik + jnp.log(total)
        occupied = occupied + mask_now[:, None, None] * alpha
        return (alpha, loglik, occupied), alpha

    alpha0 = jnp.broadcast_to(start, (persons, kinds, states)).astype(jnp.float32)
    carry0 = (alpha0, jnp.zeros((persons, kinds), jnp.float32), jnp.zeros((persons, kinds, states), jnp.float32))
    (alpha, loglik, occupied), history = lax.scan(advance, carry0, (jnp.transpose(emis, (1, 0, 2, 3)), observed_f.T))
    filtered = jnp.transpose(history, (1, 0, 2, 3))
    loglik_rate = loglik / epochs
    type_post = jax.nn.softmax(type_prior[None, :] + 8.0 * loglik_rate, axis=-1)
    numer = jnp.einsum('pk,pks->ks', type_post, occupied, precision=lax.Precision.HIGHEST)
    denom = jnp.einsum('pk,p->k', type_post, jnp.sum(observed_f, axis=1), precision=lax.Precision.HIGHEST)
    occupancy = numer / denom[:, None]
    return (loglik_rate, type_post, occupancy, filtered)
```

```python
import jax
import jax.numpy as jnp
from jax import lax
from jax.sharding import PartitionSpec as P

HIGHEST = lax.Precision.HIGHEST
HIGH = lax.Precision.HIGH


def padded(block, sides, width):
    for axis, dim in sides:
        count = lax.axis_size(axis)
        forward = [(i, i + 1) for i in range(count - 1)]
        backward = [(target, source) for source, target in forward]
        low = lax.ppermute(
            lax.slice_in_dim(block, block.shape[dim] - width, None, axis=dim), axis, forward
        )
        high = lax.ppermute(lax.slice_in_dim(block, 0, width, axis=dim), axis, backward)
        block = jnp.concatenate([low, block, high], axis=dim)
    return block


def norm_mat(m):
    return m / jnp.sum(m, axis=(-2, -1), keepdims=True)


def norm_vec(v):
    return v / jnp.sum(v, axis=-1, keepdims=True)


def mat_mat(a, b):
    return jnp.einsum("...im,...ml->...il", a, b, precision=HIGH)


def shift_in(x, axis, step, fill):
    count = lax.axis_size(axis)
    if step >= count:
        return jnp.broadcast_to(fill, x.shape)
    moved = lax.ppermute(x, axis, [(i, i + step) for i in range(count - step)])
    return jnp.where(lax.axis_index(axis) >= step, moved, fill)


def exclusive_scan(mats, axis):
    count = lax.axis_size(axis)
    eye = jnp.eye(mats.shape[-1], dtype=mats.dtype)
    one = shift_in(mats, axis, 1, eye)
    two = shift_in(mats, axis, 2, eye)
    acc = norm_mat(mat_mat(two, one))
    step = 2
    while step < count:
        acc = norm_mat(mat_mat(shift_in(acc, axis, step, eye), acc))
        step *= 2
    return acc


def butterfly_sum(x, axes):
    for axis in axes:
        count = lax.axis_size(axis)
        bit = 1
        while bit < count:
            x = x + lax.ppermute(x, axis, [(i, i ^ bit) for i in range(count)])
            bit *= 2
    return x


def on_device(
    features,
    wear,
    rec_start,
    rec_end,
    conv_first,
    conv_second,
    emit_weight,
    leave,
    jump,
    init_logits,
    type_prior,
):
    persons = features.shape[1]
    span = features.shape[2]
    kinds = jump.shape[0]
    states = jump.shape[-1]
    tm_index = lax.axis_index("tm")
    type_index = lax.axis_index("type")
    people_index = lax.axis_index("people")
    total_epochs = span * lax.axis_size("tm")
    extended = padded(features, (("tm", 2),), 5)
    first = jnp.zeros((persons, span + 8, conv_first.shape[2]), jnp.float32)
    for tap in range(3):
        first = first + jnp.einsum(
            "ipt,ic->ptc",
            extended[:, :, tap : tap + span + 8],
            conv_first[tap],
            preferred_element_type=jnp.float32,
        )
    wide_pos = tm_index * span - 4 + jnp.arange(span + 8, dtype=jnp.int32)
    inside = (wide_pos >= 0) & (wide_pos < total_epochs)
    first = jnp.where(inside[None, :, None], jax.nn.silu(first), 0.0).astype(jnp.bfloat16)
    second = jnp.zeros((persons, span, conv_second.shape[2]), jnp.float32)
    for tap in range(3):
        second = second + jnp.einsum(
            "ptc,cd->ptd",
            first[:, 4 * tap : 4 * tap + span],
            conv_second[tap],
            preferred_element_type=jnp.float32,
        )
    second = jax.nn.silu(second).astype(jnp.bfloat16)
    logits = jnp.einsum("ptc,cm->ptm", second, emit_weight, preferred_element_type=jnp.float32)
    probs = jnp.exp(jax.nn.log_softmax(logits.reshape(persons, span, kinds, states), axis=-1))
    positions = tm_index * span + jnp.arange(span, dtype=jnp.int32)
    observed = (
        (wear > 0)
        & (positions[None, :] >= rec_start[:, None])
        & (positions[None, :] < rec_end[:, None])
    )
    emis = jnp.where(observed[:, :, None, None], probs, jnp.float32(1.0))
    observed_f = observed.astype(jnp.float32)
    eye_small = jnp.eye(states, dtype=jnp.float32)
    trans = (1.0 - leave)[..., None] * eye_small + leave[..., None] * jax.nn.softmax(jump, axis=-1)
    start = jax.nn.softmax(init_logits, axis=-1)

    pairs = emis.reshape(persons, span // 2, 2, kinds, states)
    e_even = pairs[:, :, 0]
    e_odd = pairs[:, :, 1]
    left = trans[None, None] * e_even[:, :, :, None, :]
    level = jnp.einsum("pjkim,kml->pjkil", left, trans, precision=HIGH) * e_odd[:, :, :, None, :]
    levels = [None, norm_mat(level)]
    while levels[-1].shape[1] > 1:
        last = levels[-1]
        halves = last.reshape((persons, last.shape[1] // 2, 2) + last.shape[2:])
        levels.append(norm_mat(mat_mat(halves[:, :, 0], halves[:, :, 1])))
    device_op = levels[-1][:, 0]

    before = exclusive_scan(device_op, "tm")
    alpha_in = norm_vec(jnp.einsum("ki,pkij->pkj", start, before, precision=HIGHEST))

    entry = alpha_in[:, None]
    for depth in range(len(levels) - 1, 1, -1):
        sibling = levels[depth - 1].reshape(
            (persons, entry.shape[1], 2) + levels[depth - 1].shape[2:]
        )[:, :, 0]
        moved = norm_vec(jnp.einsum("pnki,pnkil->pnkl", entry, sibling, precision=HIGHEST))
        entry = jnp.stack([entry, moved], axis=2).reshape(
            persons, 2 * entry.shape[1], kinds, states
        )
    u = jnp.einsum("pjki,kil->pjkl", entry, trans, precision=HIGHEST) * e_even
    c_even = jnp.sum(u, axis=-1)
    a_even = u / c_even[..., None]
    v = jnp.einsum("pjki,kil->pjkl", a_even, trans, precision=HIGHEST) * e_odd
    c_odd = jnp.sum(v, axis=-1)
    a_odd = v / c_odd[..., None]
    filtered = jnp.stack([a_even, a_odd], axis=2).reshape(persons, span, kinds, states)
    own_log = jnp.sum(jnp.log(c_even), axis=1) + jnp.sum(jnp.log(c_odd), axis=1)
    occupied = jnp.einsum("pt,ptks->pks", observed_f, filtered, precision=HIGHEST)
    count = jnp.sum(observed_f, axis=1)

    halves_n = lax.axis_size("type")
    people_n = lax.axis_size("people") * persons
    row = jnp.concatenate(
        [own_log, occupied.reshape(persons, kinds * states), count[:, None]], axis=1
    )
    person_hot = (
        people_index * persons + jnp.arange(persons)[:, None] == jnp.arange(people_n)[None, :]
    ).astype(jnp.float32)
    half_hot = (type_index == jnp.arange(halves_n)).astype(jnp.float32)
    table = person_hot[:, :, None, None] * half_hot[None, None, :, None] * row[:, None, None, :]
    table = butterfly_sum(jnp.sum(table, axis=0), ("type", "people", "tm"))

    full = table[:, :, :kinds].reshape(people_n, halves_n * kinds)
    rate_full = full / total_epochs
    post_full = jax.nn.softmax(type_prior[None, :] + 8.0 * rate_full, axis=-1)
    offset = type_index * kinds
    mine = people_index * persons
    rate_own = lax.dynamic_slice(rate_full, (mine, offset), (persons, kinds))
    post_own = lax.dynamic_slice(post_full, (mine, offset), (persons, kinds))
    post_type = lax.dynamic_slice(post_full, (jnp.int32(0), offset), (people_n, kinds))
    occ_all = jnp.take(table, type_index, axis=1)[:, kinds : kinds + kinds * states]
    occ_all = occ_all.reshape(people_n, kinds, states)
    cnt_all = jnp.take(table, type_index, axis=1)[:, kinds + kinds * states]
    numer = jnp.einsum("pk,pks->ks", post_type, occ_all, precision=HIGHEST)
    denom = jnp.einsum("pk,p->k", post_type, cnt_all, precision=HIGHEST)
    occupancy = numer / denom[:, None]
    return (rate_own, post_own, occupancy, filtered)


def solution(mesh):
    return jax.shard_map(
        on_device,
        mesh=mesh,
        in_specs=(
            P(None, "people", "tm"),
            P("people", "tm"),
            P("people"),
            P("people"),
            P(),
            P(),
            P(None, "type"),
            P("type", None),
            P("type", None, None),
            P("type", None),
            P(),
        ),
        out_specs=(
            P("people", "type"),
            P("people", "type"),
            P("type", None),
            P("people", "tm", "type", None),
        ),
        check_vma=False,
    )
```

```python
import jax
import jax.numpy as jnp
from jax import lax
from jax.sharding import PartitionSpec as P

HIGHEST = lax.Precision.HIGHEST
HIGH = lax.Precision.HIGH


def padded(block, sides, width):
    for axis, dim in sides:
        count = lax.axis_size(axis)
        forward = [(i, i + 1) for i in range(count - 1)]
        backward = [(target, source) for source, target in forward]
        low = lax.ppermute(
            lax.slice_in_dim(block, block.shape[dim] - width, None, axis=dim), axis, forward
        )
        high = lax.ppermute(lax.slice_in_dim(block, 0, width, axis=dim), axis, backward)
        block = jnp.concatenate([low, block, high], axis=dim)
    return block


def norm_mat(m):
    return m / jnp.sum(m, axis=(-2, -1), keepdims=True)


def norm_vec(v):
    return v / jnp.sum(v, axis=-1, keepdims=True)


def mat_mat(a, b):
    return jnp.einsum("...im,...ml->...il", a, b, precision=HIGH)


def shift_in(x, axis, step, fill):
    count = lax.axis_size(axis)
    if step >= count:
        return jnp.broadcast_to(fill, x.shape)
    moved = lax.ppermute(x, axis, [(i, i + step) for i in range(count - step)])
    return jnp.where(lax.axis_index(axis) >= step, moved, fill)


def chain(mats):
    while len(mats) > 1:
        half = len(mats) // 2
        left = jnp.stack(mats[0 : 2 * half : 2])
        right = jnp.stack(mats[1 : 2 * half : 2])
        joined = norm_mat(mat_mat(left, right))
        mats = [joined[i] for i in range(half)] + mats[2 * half :]
    return mats[0]


def exclusive_scan(mats, axis, radix):
    count = lax.axis_size(axis)
    eye = jnp.eye(mats.shape[-1], dtype=mats.dtype)
    width = min(radix, count)
    acc = chain([shift_in(mats, axis, width - m, eye) for m in range(width)])
    step = width
    while step < count:
        width = min(radix, count // step)
        parts = [shift_in(acc, axis, (width - 1 - m) * step, eye) for m in range(width - 1)]
        acc = chain(parts + [acc])
        step *= width
    return acc


def butterfly_sum(x, axis, count, radix):
    step = 1
    while step < count:
        width = min(radix, count // step)
        total = x
        for m in range(1, width):
            pairs = []
            for i in range(count):
                digit = (i // step) % width
                pairs.append((i, i + ((digit + m) % width - digit) * step))
            total = total + lax.ppermute(x, axis, pairs)
        x = total
        step *= width
    return x


def on_device(
    features,
    wear,
    rec_start,
    rec_end,
    conv_first,
    conv_second,
    emit_weight,
    leave,
    jump,
    init_logits,
    type_prior,
):
    persons = features.shape[1]
    span = features.shape[2]
    kinds = jump.shape[0]
    states = jump.shape[-1]
    tm_index = lax.axis_index("tm")
    type_index = lax.axis_index("type")
    people_index = lax.axis_index("people")
    total_epochs = span * lax.axis_size("tm")
    extended = padded(features, (("tm", 2),), 5)
    first = jnp.zeros((persons, span + 8, conv_first.shape[2]), jnp.float32)
    for tap in range(3):
        first = first + jnp.einsum(
            "ipt,ic->ptc",
            extended[:, :, tap : tap + span + 8],
            conv_first[tap],
            preferred_element_type=jnp.float32,
        )
    wide_pos = tm_index * span - 4 + jnp.arange(span + 8, dtype=jnp.int32)
    inside = (wide_pos >= 0) & (wide_pos < total_epochs)
    first = jnp.where(inside[None, :, None], jax.nn.silu(first), 0.0).astype(jnp.bfloat16)
    second = jnp.zeros((persons, span, conv_second.shape[2]), jnp.float32)
    for tap in range(3):
        second = second + jnp.einsum(
            "ptc,cd->ptd",
            first[:, 4 * tap : 4 * tap + span],
            conv_second[tap],
            preferred_element_type=jnp.float32,
        )
    second = jax.nn.silu(second).astype(jnp.bfloat16)
    logits = jnp.einsum("ptc,cm->ptm", second, emit_weight, preferred_element_type=jnp.float32)
    probs = jnp.exp(jax.nn.log_softmax(logits.reshape(persons, span, kinds, states), axis=-1))
    positions = tm_index * span + jnp.arange(span, dtype=jnp.int32)
    observed = (
        (wear > 0)
        & (positions[None, :] >= rec_start[:, None])
        & (positions[None, :] < rec_end[:, None])
    )
    emis = jnp.where(observed[:, :, None, None], probs, jnp.float32(1.0))
    observed_f = observed.astype(jnp.float32)
    eye_small = jnp.eye(states, dtype=jnp.float32)
    trans = (1.0 - leave)[..., None] * eye_small + leave[..., None] * jax.nn.softmax(jump, axis=-1)
    start = jax.nn.softmax(init_logits, axis=-1)

    pairs = emis.reshape(persons, span // 2, 2, kinds, states)
    e_even = pairs[:, :, 0]
    e_odd = pairs[:, :, 1]
    left = trans[None, None] * e_even[:, :, :, None, :]
    level = jnp.einsum("pjkim,kml->pjkil", left, trans, precision=HIGH) * e_odd[:, :, :, None, :]
    levels = [None, norm_mat(level)]
    while levels[-1].shape[1] > 1:
        last = levels[-1]
        halves = last.reshape((persons, last.shape[1] // 2, 2) + last.shape[2:])
        levels.append(norm_mat(mat_mat(halves[:, :, 0], halves[:, :, 1])))
    device_op = levels[-1][:, 0]

    before = exclusive_scan(device_op, "tm", 4)
    alpha_in = norm_vec(jnp.einsum("ki,pkij->pkj", start, before, precision=HIGHEST))

    entry = alpha_in[:, None]
    for depth in range(len(levels) - 1, 1, -1):
        sibling = levels[depth - 1].reshape(
            (persons, entry.shape[1], 2) + levels[depth - 1].shape[2:]
        )[:, :, 0]
        moved = norm_vec(jnp.einsum("pnki,pnkil->pnkl", entry, sibling, precision=HIGHEST))
        entry = jnp.stack([entry, moved], axis=2).reshape(
            persons, 2 * entry.shape[1], kinds, states
        )
    u = jnp.einsum("pjki,kil->pjkl", entry, trans, precision=HIGHEST) * e_even
    c_even = jnp.sum(u, axis=-1)
    a_even = u / c_even[..., None]
    v = jnp.einsum("pjki,kil->pjkl", a_even, trans, precision=HIGHEST) * e_odd
    c_odd = jnp.sum(v, axis=-1)
    a_odd = v / c_odd[..., None]
    filtered = jnp.stack([a_even, a_odd], axis=2).reshape(persons, span, kinds, states)
    own_log = jnp.sum(jnp.log(c_even), axis=1) + jnp.sum(jnp.log(c_odd), axis=1)
    occupied = jnp.einsum("pt,ptks->pks", observed_f, filtered, precision=HIGHEST)
    count = jnp.sum(observed_f, axis=1)

    halves_n = lax.axis_size("type")
    people_n = lax.axis_size("people") * persons
    row = jnp.concatenate(
        [own_log, occupied.reshape(persons, kinds * states), count[:, None]], axis=1
    )
    person_hot = (
        people_index * persons + jnp.arange(persons)[:, None] == jnp.arange(people_n)[None, :]
    ).astype(jnp.float32)
    half_hot = (type_index == jnp.arange(halves_n)).astype(jnp.float32)
    table = person_hot[:, :, None, None] * half_hot[None, None, :, None] * row[:, None, None, :]
    table = jnp.sum(table, axis=0)
    table = butterfly_sum(table, ("people", "type"), people_n // persons * halves_n, 4)
    table = butterfly_sum(table, "tm", lax.axis_size("tm"), 4)

    full = table[:, :, :kinds].reshape(people_n, halves_n * kinds)
    rate_full = full / total_epochs
    post_full = jax.nn.softmax(type_prior[None, :] + 8.0 * rate_full, axis=-1)
    offset = type_index * kinds
    mine = people_index * persons
    rate_own = lax.dynamic_slice(rate_full, (mine, offset), (persons, kinds))
    post_own = lax.dynamic_slice(post_full, (mine, offset), (persons, kinds))
    post_type = lax.dynamic_slice(post_full, (jnp.int32(0), offset), (people_n, kinds))
    occ_all = jnp.take(table, type_index, axis=1)[:, kinds : kinds + kinds * states]
    occ_all = occ_all.reshape(people_n, kinds, states)
    cnt_all = jnp.take(table, type_index, axis=1)[:, kinds + kinds * states]
    numer = jnp.einsum("pk,pks->ks", post_type, occ_all, precision=HIGHEST)
    denom = jnp.einsum("pk,p->k", post_type, cnt_all, precision=HIGHEST)
    occupancy = numer / denom[:, None]
    return (rate_own, post_own, occupancy, filtered)


def solution(mesh):
    return jax.shard_map(
        on_device,
        mesh=mesh,
        in_specs=(
            P(None, "people", "tm"),
            P("people", "tm"),
            P("people"),
            P("people"),
            P(),
            P(),
            P(None, "type"),
            P("type", None),
            P("type", None, None),
            P("type", None),
            P(),
        ),
        out_specs=(
            P("people", "type"),
            P("people", "type"),
            P("type", None),
            P("people", "tm", "type", None),
        ),
        check_vma=False,
    )
```

```python
import jax
import jax.numpy as jnp
from jax import lax
from jax.sharding import PartitionSpec as P

HIGHEST = lax.Precision.HIGHEST
HIGH = lax.Precision.HIGH
TM_SPLIT = (8, 4, 2)
TM = ("tz", "ty", "tc")


def padded(block, sides, width):
    for axis, dim in sides:
        count = 1
        for name in axis:
            count *= lax.axis_size(name)
        forward = [(i, i + 1) for i in range(count - 1)]
        backward = [(target, source) for source, target in forward]
        low = lax.ppermute(
            lax.slice_in_dim(block, block.shape[dim] - width, None, axis=dim), axis, forward
        )
        high = lax.ppermute(lax.slice_in_dim(block, 0, width, axis=dim), axis, backward)
        block = jnp.concatenate([low, block, high], axis=dim)
    return block


def norm_mat(m):
    return m / jnp.sum(m, axis=(-2, -1), keepdims=True)


def norm_vec(v):
    return v / jnp.sum(v, axis=-1, keepdims=True)


def mat_mat(a, b):
    return jnp.einsum("...im,...ml->...il", a, b, precision=HIGH)


def chain(mats):
    while len(mats) > 1:
        half = len(mats) // 2
        left = jnp.stack(mats[0 : 2 * half : 2])
        right = jnp.stack(mats[1 : 2 * half : 2])
        joined = norm_mat(mat_mat(left, right))
        mats = [joined[i] for i in range(half)] + mats[2 * half :]
    return mats[0]


def group_scan(mats, axis, whole=True):
    count = lax.axis_size(axis)
    mine = lax.axis_index(axis)
    eye = jnp.eye(mats.shape[-1], dtype=mats.dtype)
    everyone = lax.all_gather(mats, axis)
    earlier = [jnp.where(mine > j, everyone[j], eye) for j in range(count)]
    if not whole:
        return chain(earlier), None
    both = chain([jnp.stack([earlier[j], everyone[j]]) for j in range(count)])
    return both[0], both[1]


def exclusive_scan(mats, axes):
    parts = []
    for depth, axis in enumerate(reversed(axes)):
        before, mats = group_scan(mats, axis, depth < len(axes) - 1)
        parts.append(before)
    return chain(parts[::-1])


def on_device(
    features,
    wear,
    rec_start,
    rec_end,
    conv_first,
    conv_second,
    emit_weight,
    leave,
    jump,
    init_logits,
    type_prior,
):
    persons = features.shape[1]
    span = features.shape[2]
    kinds = jump.shape[0]
    states = jump.shape[-1]
    tm_index = lax.axis_index(TM)
    type_index = lax.axis_index("type")
    people_index = lax.axis_index("people")
    tm_count = 1
    for axis in TM:
        tm_count *= lax.axis_size(axis)
    total_epochs = span * tm_count
    extended = padded(features, ((TM, 2),), 5)
    first = jnp.zeros((persons, span + 8, conv_first.shape[2]), jnp.float32)
    for tap in range(3):
        first = first + jnp.einsum(
            "ipt,ic->ptc",
            extended[:, :, tap : tap + span + 8],
            conv_first[tap],
            preferred_element_type=jnp.float32,
        )
    wide_pos = tm_index * span - 4 + jnp.arange(span + 8, dtype=jnp.int32)
    inside = (wide_pos >= 0) & (wide_pos < total_epochs)
    first = jnp.where(inside[None, :, None], jax.nn.silu(first), 0.0).astype(jnp.bfloat16)
    second = jnp.zeros((persons, span, conv_second.shape[2]), jnp.float32)
    for tap in range(3):
        second = second + jnp.einsum(
            "ptc,cd->ptd",
            first[:, 4 * tap : 4 * tap + span],
            conv_second[tap],
            preferred_element_type=jnp.float32,
        )
    second = jax.nn.silu(second).astype(jnp.bfloat16)
    logits = jnp.einsum("ptc,cm->ptm", second, emit_weight, preferred_element_type=jnp.float32)
    probs = jnp.exp(jax.nn.log_softmax(logits.reshape(persons, span, kinds, states), axis=-1))
    positions = tm_index * span + jnp.arange(span, dtype=jnp.int32)
    observed = (
        (wear > 0)
        & (positions[None, :] >= rec_start[:, None])
        & (positions[None, :] < rec_end[:, None])
    )
    emis = jnp.where(observed[:, :, None, None], probs, jnp.float32(1.0))
    observed_f = observed.astype(jnp.float32)
    eye_small = jnp.eye(states, dtype=jnp.float32)
    trans = (1.0 - leave)[..., None] * eye_small + leave[..., None] * jax.nn.softmax(jump, axis=-1)
    start = jax.nn.softmax(init_logits, axis=-1)

    pairs = emis.reshape(persons, span // 2, 2, kinds, states)
    e_even = pairs[:, :, 0]
    e_odd = pairs[:, :, 1]
    left = trans[None, None] * e_even[:, :, :, None, :]
    level = jnp.einsum("pjkim,kml->pjkil", left, trans, precision=HIGH) * e_odd[:, :, :, None, :]
    levels = [None, norm_mat(level)]
    while levels[-1].shape[1] > 1:
        last = levels[-1]
        halves = last.reshape((persons, last.shape[1] // 2, 2) + last.shape[2:])
        levels.append(norm_mat(mat_mat(halves[:, :, 0], halves[:, :, 1])))
    device_op = levels[-1][:, 0]

    before = exclusive_scan(device_op, TM)
    alpha_in = norm_vec(jnp.einsum("ki,pkij->pkj", start, before, precision=HIGHEST))

    entry = alpha_in[:, None]
    for depth in range(len(levels) - 1, 1, -1):
        sibling = levels[depth - 1].reshape(
            (persons, entry.shape[1], 2) + levels[depth - 1].shape[2:]
        )[:, :, 0]
        moved = norm_vec(jnp.einsum("pnki,pnkil->pnkl", entry, sibling, precision=HIGHEST))
        entry = jnp.stack([entry, moved], axis=2).reshape(
            persons, 2 * entry.shape[1], kinds, states
        )
    u = jnp.einsum("pjki,kil->pjkl", entry, trans, precision=HIGHEST) * e_even
    c_even = jnp.sum(u, axis=-1)
    a_even = u / c_even[..., None]
    v = jnp.einsum("pjki,kil->pjkl", a_even, trans, precision=HIGHEST) * e_odd
    c_odd = jnp.sum(v, axis=-1)
    a_odd = v / c_odd[..., None]
    filtered = jnp.stack([a_even, a_odd], axis=2).reshape(persons, span, kinds, states)
    own_log = jnp.sum(jnp.log(c_even), axis=1) + jnp.sum(jnp.log(c_odd), axis=1)
    occupied = jnp.einsum("pt,ptks->pks", observed_f, filtered, precision=HIGHEST)
    count = jnp.sum(observed_f, axis=1)

    halves_n = lax.axis_size("type")
    people_n = lax.axis_size("people") * persons
    row = jnp.concatenate(
        [own_log, occupied.reshape(persons, kinds * states), count[:, None]], axis=1
    )
    person_hot = (
        people_index * persons + jnp.arange(persons)[:, None] == jnp.arange(people_n)[None, :]
    ).astype(jnp.float32)
    half_hot = (type_index == jnp.arange(halves_n)).astype(jnp.float32)
    table = person_hot[:, :, None, None] * half_hot[None, None, :, None] * row[:, None, None, :]
    table = jnp.sum(table, axis=0)
    for axis in TM[::-1] + ("people", "type"):
        table = lax.psum(table, axis)

    full = table[:, :, :kinds].reshape(people_n, halves_n * kinds)
    rate_full = full / total_epochs
    post_full = jax.nn.softmax(type_prior[None, :] + 8.0 * rate_full, axis=-1)
    offset = type_index * kinds
    mine = people_index * persons
    rate_own = lax.dynamic_slice(rate_full, (mine, offset), (persons, kinds))
    post_own = lax.dynamic_slice(post_full, (mine, offset), (persons, kinds))
    post_type = lax.dynamic_slice(post_full, (jnp.int32(0), offset), (people_n, kinds))
    occ_all = jnp.take(table, type_index, axis=1)[:, kinds : kinds + kinds * states]
    occ_all = occ_all.reshape(people_n, kinds, states)
    cnt_all = jnp.take(table, type_index, axis=1)[:, kinds + kinds * states]
    numer = jnp.einsum("pk,pks->ks", post_type, occ_all, precision=HIGHEST)
    denom = jnp.einsum("pk,p->k", post_type, cnt_all, precision=HIGHEST)
    occupancy = numer / denom[:, None]
    return (rate_own, post_own, occupancy, filtered)


def solution(mesh):
    people, epochs, halves = mesh.devices.shape
    assert epochs == TM_SPLIT[0] * TM_SPLIT[1] * TM_SPLIT[2]
    fine = jax.sharding.Mesh(
        mesh.devices.reshape((people,) + TM_SPLIT + (halves,)), ("people",) + TM + ("type",)
    )
    return jax.shard_map(
        on_device,
        mesh=fine,
        in_specs=(
            P(None, "people", TM),
            P("people", TM),
            P("people"),
            P("people"),
            P(),
            P(),
            P(None, "type"),
            P("type", None),
            P("type", None, None),
            P("type", None),
            P(),
        ),
        out_specs=(
            P("people", "type"),
            P("people", "type"),
            P("type", None),
            P("people", TM, "type", None),
        ),
        check_vma=False,
    )
```

```python
import jax
import jax.numpy as jnp
from jax import lax
from jax.sharding import PartitionSpec as P

HIGHEST = lax.Precision.HIGHEST
HIGH = lax.Precision.HIGH
TM_SPLIT = (8, 4, 2)
TM = ("tz", "ty", "tc")


def padded(block, sides, width):
    for axis, dim in sides:
        count = 1
        for name in axis:
            count *= lax.axis_size(name)
        forward = [(i, i + 1) for i in range(count - 1)]
        backward = [(target, source) for source, target in forward]
        low = lax.ppermute(
            lax.slice_in_dim(block, block.shape[dim] - width, None, axis=dim), axis, forward
        )
        high = lax.ppermute(lax.slice_in_dim(block, 0, width, axis=dim), axis, backward)
        block = jnp.concatenate([low, block, high], axis=dim)
    return block


def norm_mat(m):
    return m / jnp.sum(m, axis=(-2, -1), keepdims=True)


def norm_vec(v):
    return v / jnp.sum(v, axis=-1, keepdims=True)


def mat_mat(a, b):
    return jnp.einsum("...im,...ml->...il", a, b, precision=HIGH)


def bit_reverse(x, axis):
    bits = x.shape[axis].bit_length() - 1
    split = x.shape[:axis] + (2,) * bits + x.shape[axis + 1 :]
    perm = (
        list(range(axis))
        + [axis + bits - 1 - i for i in range(bits)]
        + list(range(axis + bits, len(split)))
    )
    return jnp.transpose(x.reshape(split), perm).reshape(x.shape)


def chain(mats):
    while len(mats) > 1:
        half = len(mats) // 2
        left = jnp.stack(mats[0 : 2 * half : 2])
        right = jnp.stack(mats[1 : 2 * half : 2])
        joined = norm_mat(mat_mat(left, right))
        mats = [joined[i] for i in range(half)] + mats[2 * half :]
    return mats[0]


def group_scan(mats, axis, whole=True):
    count = lax.axis_size(axis)
    mine = lax.axis_index(axis)
    eye = jnp.eye(mats.shape[-1], dtype=mats.dtype)
    everyone = lax.all_gather(mats, axis)
    earlier = [jnp.where(mine > j, everyone[j], eye) for j in range(count)]
    if not whole:
        return chain(earlier), None
    both = chain([jnp.stack([earlier[j], everyone[j]]) for j in range(count)])
    return both[0], both[1]


def exclusive_scan(mats, axes):
    parts = []
    for depth, axis in enumerate(reversed(axes)):
        before, mats = group_scan(mats, axis, depth < len(axes) - 1)
        parts.append(before)
    return chain(parts[::-1])


def on_device(
    features,
    wear,
    rec_start,
    rec_end,
    conv_first,
    conv_second,
    emit_weight,
    leave,
    jump,
    init_logits,
    type_prior,
):
    persons = features.shape[1]
    span = features.shape[2]
    kinds = jump.shape[0]
    states = jump.shape[-1]
    tm_index = lax.axis_index(TM)
    type_index = lax.axis_index("type")
    people_index = lax.axis_index("people")
    tm_count = 1
    for axis in TM:
        tm_count *= lax.axis_size(axis)
    total_epochs = span * tm_count
    extended = padded(features, ((TM, 2),), 5)
    first = jnp.zeros((persons, span + 8, conv_first.shape[2]), jnp.float32)
    for tap in range(3):
        first = first + jnp.einsum(
            "ipt,ic->ptc",
            extended[:, :, tap : tap + span + 8],
            conv_first[tap],
            preferred_element_type=jnp.float32,
        )
    wide_pos = tm_index * span - 4 + jnp.arange(span + 8, dtype=jnp.int32)
    inside = (wide_pos >= 0) & (wide_pos < total_epochs)
    first = jnp.where(inside[None, :, None], jax.nn.silu(first), 0.0).astype(jnp.bfloat16)
    second = jnp.zeros((persons, span, conv_second.shape[2]), jnp.float32)
    for tap in range(3):
        second = second + jnp.einsum(
            "ptc,cd->ptd",
            first[:, 4 * tap : 4 * tap + span],
            conv_second[tap],
            preferred_element_type=jnp.float32,
        )
    second = jax.nn.silu(second).astype(jnp.bfloat16)
    logits = jnp.einsum("ptc,cm->ptm", second, emit_weight, preferred_element_type=jnp.float32)
    probs = jnp.exp(jax.nn.log_softmax(logits.reshape(persons, span, kinds, states), axis=-1))
    positions = tm_index * span + jnp.arange(span, dtype=jnp.int32)
    observed = (
        (wear > 0)
        & (positions[None, :] >= rec_start[:, None])
        & (positions[None, :] < rec_end[:, None])
    )
    emis = jnp.where(observed[:, :, None, None], probs, jnp.float32(1.0))
    observed_f = observed.astype(jnp.float32)
    eye_small = jnp.eye(states, dtype=jnp.float32)
    trans = (1.0 - leave)[..., None] * eye_small + leave[..., None] * jax.nn.softmax(jump, axis=-1)
    start = jax.nn.softmax(init_logits, axis=-1)

    order = bit_reverse(jnp.transpose(emis, (2, 0, 1, 3)), 2)
    half = span // 2
    e_even = order[:, :, :half]
    e_odd = order[:, :, half:]
    left = trans[:, None, None] * e_even[:, :, :, None, :]
    level = jnp.einsum("kpjim,kml->kpjil", left, trans, precision=HIGH) * e_odd[:, :, :, None, :]
    levels = [None, norm_mat(level)]
    while levels[-1].shape[2] > 1:
        last = levels[-1]
        n = last.shape[2] // 2
        levels.append(norm_mat(mat_mat(last[:, :, :n], last[:, :, n:])))
    device_op = levels[-1][:, :, 0]

    before = exclusive_scan(device_op, TM)
    alpha_in = norm_vec(jnp.einsum("ki,kpij->kpj", start, before, precision=HIGHEST))

    entry = alpha_in[:, :, None]
    for depth in range(len(levels) - 1, 1, -1):
        n = entry.shape[2]
        sibling = levels[depth - 1][:, :, :n]
        moved = norm_vec(jnp.einsum("kpni,kpnil->kpnl", entry, sibling, precision=HIGHEST))
        entry = jnp.concatenate([entry, moved], axis=2)
    u = jnp.einsum("kpji,kil->kpjl", entry, trans, precision=HIGHEST) * e_even
    c_even = jnp.sum(u, axis=-1)
    a_even = u / c_even[..., None]
    v = jnp.einsum("kpji,kil->kpjl", a_even, trans, precision=HIGHEST) * e_odd
    c_odd = jnp.sum(v, axis=-1)
    a_odd = v / c_odd[..., None]
    alpha = bit_reverse(jnp.concatenate([a_even, a_odd], axis=2), 2)
    filtered = jnp.transpose(alpha, (1, 2, 0, 3))
    own_log = jnp.transpose(jnp.sum(jnp.log(c_even), axis=2) + jnp.sum(jnp.log(c_odd), axis=2))
    occupied = jnp.einsum("pt,ptks->pks", observed_f, filtered, precision=HIGHEST)
    count = jnp.sum(observed_f, axis=1)

    halves_n = lax.axis_size("type")
    people_n = lax.axis_size("people") * persons
    row = jnp.concatenate(
        [own_log, occupied.reshape(persons, kinds * states), count[:, None]], axis=1
    )
    person_hot = (
        people_index * persons + jnp.arange(persons)[:, None] == jnp.arange(people_n)[None, :]
    ).astype(jnp.float32)
    half_hot = (type_index == jnp.arange(halves_n)).astype(jnp.float32)
    table = person_hot[:, :, None, None] * half_hot[None, None, :, None] * row[:, None, None, :]
    table = jnp.sum(table, axis=0)
    for axis in TM[::-1] + (("people", "type"),):
        table = lax.psum(table, axis)

    full = table[:, :, :kinds].reshape(people_n, halves_n * kinds)
    rate_full = full / total_epochs
    post_full = jax.nn.softmax(type_prior[None, :] + 8.0 * rate_full, axis=-1)
    offset = type_index * kinds
    mine = people_index * persons
    rate_own = lax.dynamic_slice(rate_full, (mine, offset), (persons, kinds))
    post_own = lax.dynamic_slice(post_full, (mine, offset), (persons, kinds))
    post_type = lax.dynamic_slice(post_full, (jnp.int32(0), offset), (people_n, kinds))
    occ_all = jnp.take(table, type_index, axis=1)[:, kinds : kinds + kinds * states]
    occ_all = occ_all.reshape(people_n, kinds, states)
    cnt_all = jnp.take(table, type_index, axis=1)[:, kinds + kinds * states]
    numer = jnp.einsum("pk,pks->ks", post_type, occ_all, precision=HIGHEST)
    denom = jnp.einsum("pk,p->k", post_type, cnt_all, precision=HIGHEST)
    occupancy = numer / denom[:, None]
    return (rate_own, post_own, occupancy, filtered)


def solution(mesh):
    people, epochs, halves = mesh.devices.shape
    assert epochs == TM_SPLIT[0] * TM_SPLIT[1] * TM_SPLIT[2]
    fine = jax.sharding.Mesh(
        mesh.devices.reshape((people,) + TM_SPLIT + (halves,)), ("people",) + TM + ("type",)
    )
    return jax.shard_map(
        on_device,
        mesh=fine,
        in_specs=(
            P(None, "people", TM),
            P("people", TM),
            P("people"),
            P("people"),
            P(),
            P(),
            P(None, "type"),
            P("type", None),
            P("type", None, None),
            P("type", None),
            P(),
        ),
        out_specs=(
            P("people", "type"),
            P("people", "type"),
            P("type", None),
            P("people", TM, "type", None),
        ),
        check_vma=False,
    )
```

```python
import jax
import jax.numpy as jnp
from jax import lax
from jax.sharding import PartitionSpec as P

HIGHEST = lax.Precision.HIGHEST
HIGH = lax.Precision.HIGH
TM_SPLIT = (8, 4, 2)
TM = ("tz", "ty", "tc")


def padded(block, sides, width):
    for axis, dim in sides:
        count = 1
        for name in axis:
            count *= lax.axis_size(name)
        forward = [(i, i + 1) for i in range(count - 1)]
        backward = [(target, source) for source, target in forward]
        low = lax.ppermute(
            lax.slice_in_dim(block, block.shape[dim] - width, None, axis=dim), axis, forward
        )
        high = lax.ppermute(lax.slice_in_dim(block, 0, width, axis=dim), axis, backward)
        block = jnp.concatenate([low, block, high], axis=dim)
    return block


def norm_mat(m):
    return m / jnp.sum(m, axis=(-2, -1), keepdims=True)


def norm_vec(v):
    return v / jnp.sum(v, axis=-1, keepdims=True)


def mat_mat(a, b):
    return jnp.einsum("...im,...ml->...il", a, b, precision=HIGH)


def bit_reverse(x, axis):
    bits = x.shape[axis].bit_length() - 1
    split = x.shape[:axis] + (2,) * bits + x.shape[axis + 1 :]
    perm = (
        list(range(axis))
        + [axis + bits - 1 - i for i in range(bits)]
        + list(range(axis + bits, len(split)))
    )
    return jnp.transpose(x.reshape(split), perm).reshape(x.shape)


def chain(mats):
    while len(mats) > 1:
        half = len(mats) // 2
        left = jnp.stack(mats[0 : 2 * half : 2])
        right = jnp.stack(mats[1 : 2 * half : 2])
        joined = norm_mat(mat_mat(left, right))
        mats = [joined[i] for i in range(half)] + mats[2 * half :]
    return mats[0]


def group_scan(mats, axis, whole=True):
    count = lax.axis_size(axis)
    mine = lax.axis_index(axis)
    eye = jnp.eye(mats.shape[-1], dtype=mats.dtype)
    everyone = lax.all_gather(mats, axis)
    earlier = [jnp.where(mine > j, everyone[j], eye) for j in range(count)]
    if not whole:
        return chain(earlier), None
    both = chain([jnp.stack([earlier[j], everyone[j]]) for j in range(count)])
    return both[0], both[1]


def exclusive_scan(mats, axes):
    parts = []
    for depth, axis in enumerate(reversed(axes)):
        before, mats = group_scan(mats, axis, depth < len(axes) - 1)
        parts.append(before)
    return chain(parts[::-1])


def on_device(
    features,
    wear,
    rec_start,
    rec_end,
    conv_first,
    conv_second,
    emit_weight,
    leave,
    jump,
    init_logits,
    type_prior,
):
    persons = features.shape[1]
    span = features.shape[2]
    kinds = jump.shape[0]
    states = jump.shape[-1]
    tm_index = lax.axis_index(TM)
    type_index = lax.axis_index("type")
    people_index = lax.axis_index("people")
    tm_count = 1
    for axis in TM:
        tm_count *= lax.axis_size(axis)
    total_epochs = span * tm_count
    extended = padded(features, ((TM, 2),), 5)
    first = jnp.zeros((persons, span + 8, conv_first.shape[2]), jnp.float32)
    for tap in range(3):
        first = first + jnp.einsum(
            "ipt,ic->ptc",
            extended[:, :, tap : tap + span + 8],
            conv_first[tap],
            preferred_element_type=jnp.float32,
        )
    wide_pos = tm_index * span - 4 + jnp.arange(span + 8, dtype=jnp.int32)
    inside = (wide_pos >= 0) & (wide_pos < total_epochs)
    first = jnp.where(inside[None, :, None], jax.nn.silu(first), 0.0).astype(jnp.bfloat16)
    second = jnp.zeros((persons, span, conv_second.shape[2]), jnp.float32)
    for tap in range(3):
        second = second + jnp.einsum(
            "ptc,cd->ptd",
            first[:, 4 * tap : 4 * tap + span],
            conv_second[tap],
            preferred_element_type=jnp.float32,
        )
    second = jax.nn.silu(second).astype(jnp.bfloat16)
    logits = jnp.einsum("ptc,cm->ptm", second, emit_weight, preferred_element_type=jnp.float32)
    probs = jnp.exp(jax.nn.log_softmax(logits.reshape(persons, span, kinds, states), axis=-1))
    positions = tm_index * span + jnp.arange(span, dtype=jnp.int32)
    observed = (
        (wear > 0)
        & (positions[None, :] >= rec_start[:, None])
        & (positions[None, :] < rec_end[:, None])
    )
    emis = jnp.where(observed[:, :, None, None], probs, jnp.float32(1.0))
    observed_f = observed.astype(jnp.float32)
    eye_small = jnp.eye(states, dtype=jnp.float32)
    trans = (1.0 - leave)[..., None] * eye_small + leave[..., None] * jax.nn.softmax(jump, axis=-1)
    start = jax.nn.softmax(init_logits, axis=-1)

    order = bit_reverse(jnp.transpose(emis, (2, 0, 1, 3)), 2)
    half = span // 2
    e_even = order[:, :, :half]
    e_odd = order[:, :, half:]
    quarter = span // 4
    cols = [order[:, :, m * quarter : (m + 1) * quarter, None, :] for m in range(4)]
    left = trans[:, None, None] * cols[0]
    pair = norm_mat(jnp.einsum("kpjim,kml->kpjil", left, trans, precision=HIGH) * cols[2])
    level = norm_mat(jnp.einsum("kpjim,kml->kpjil", pair, trans, precision=HIGH) * cols[1])
    level = norm_mat(jnp.einsum("kpjim,kml->kpjil", level, trans, precision=HIGH) * cols[3])
    levels = [None, pair, level]
    while levels[-1].shape[2] > 1:
        last = levels[-1]
        n = last.shape[2] // 2
        levels.append(norm_mat(mat_mat(last[:, :, :n], last[:, :, n:])))
    device_op = levels[-1][:, :, 0]

    before = exclusive_scan(device_op, TM)
    alpha_in = norm_vec(jnp.einsum("ki,kpij->kpj", start, before, precision=HIGHEST))

    entry = alpha_in[:, :, None]
    for depth in range(len(levels) - 1, 1, -1):
        n = entry.shape[2]
        sibling = levels[depth - 1][:, :, :n]
        moved = norm_vec(jnp.einsum("kpni,kpnil->kpnl", entry, sibling, precision=HIGHEST))
        entry = jnp.concatenate([entry, moved], axis=2)
    u = jnp.einsum("kpji,kil->kpjl", entry, trans, precision=HIGHEST) * e_even
    c_even = jnp.sum(u, axis=-1)
    a_even = u / c_even[..., None]
    v = jnp.einsum("kpji,kil->kpjl", a_even, trans, precision=HIGHEST) * e_odd
    c_odd = jnp.sum(v, axis=-1)
    a_odd = v / c_odd[..., None]
    alpha = bit_reverse(jnp.concatenate([a_even, a_odd], axis=2), 2)
    filtered = jnp.transpose(alpha, (1, 2, 0, 3))
    own_log = jnp.transpose(jnp.sum(jnp.log(c_even), axis=2) + jnp.sum(jnp.log(c_odd), axis=2))
    occupied = jnp.einsum("pt,ptks->pks", observed_f, filtered, precision=HIGHEST)
    count = jnp.sum(observed_f, axis=1)

    halves_n = lax.axis_size("type")
    people_n = lax.axis_size("people") * persons
    row = jnp.concatenate(
        [own_log, occupied.reshape(persons, kinds * states), count[:, None]], axis=1
    )
    person_hot = (
        people_index * persons + jnp.arange(persons)[:, None] == jnp.arange(people_n)[None, :]
    ).astype(jnp.float32)
    half_hot = (type_index == jnp.arange(halves_n)).astype(jnp.float32)
    table = person_hot[:, :, None, None] * half_hot[None, None, :, None] * row[:, None, None, :]
    table = jnp.sum(table, axis=0)
    for axis in TM[::-1] + (("people", "type"),):
        table = lax.psum(table, axis)

    full = table[:, :, :kinds].reshape(people_n, halves_n * kinds)
    rate_full = full / total_epochs
    post_full = jax.nn.softmax(type_prior[None, :] + 8.0 * rate_full, axis=-1)
    offset = type_index * kinds
    mine = people_index * persons
    rate_own = lax.dynamic_slice(rate_full, (mine, offset), (persons, kinds))
    post_own = lax.dynamic_slice(post_full, (mine, offset), (persons, kinds))
    post_type = lax.dynamic_slice(post_full, (jnp.int32(0), offset), (people_n, kinds))
    occ_all = jnp.take(table, type_index, axis=1)[:, kinds : kinds + kinds * states]
    occ_all = occ_all.reshape(people_n, kinds, states)
    cnt_all = jnp.take(table, type_index, axis=1)[:, kinds + kinds * states]
    numer = jnp.einsum("pk,pks->ks", post_type, occ_all, precision=HIGHEST)
    denom = jnp.einsum("pk,p->k", post_type, cnt_all, precision=HIGHEST)
    occupancy = numer / denom[:, None]
    return (rate_own, post_own, occupancy, filtered)


def solution(mesh):
    people, epochs, halves = mesh.devices.shape
    assert epochs == TM_SPLIT[0] * TM_SPLIT[1] * TM_SPLIT[2]
    fine = jax.sharding.Mesh(
        mesh.devices.reshape((people,) + TM_SPLIT + (halves,)), ("people",) + TM + ("type",)
    )
    return jax.shard_map(
        on_device,
        mesh=fine,
        in_specs=(
            P(None, "people", TM),
            P("people", TM),
            P("people"),
            P("people"),
            P(),
            P(),
            P(None, "type"),
            P("type", None),
            P("type", None, None),
            P("type", None),
            P(),
        ),
        out_specs=(
            P("people", "type"),
            P("people", "type"),
            P("type", None),
            P("people", TM, "type", None),
        ),
        check_vma=False,
    )
```

```python
import jax
import jax.numpy as jnp
from jax import lax
from jax.sharding import PartitionSpec as P

HIGHEST = lax.Precision.HIGHEST
HIGH = lax.Precision.HIGH
TM_SPLIT = (8, 4, 2)
TM = ("tz", "ty", "tc")


def padded(block, sides, width):
    for axis, dim in sides:
        count = 1
        for name in axis:
            count *= lax.axis_size(name)
        forward = [(i, i + 1) for i in range(count - 1)]
        backward = [(target, source) for source, target in forward]
        low = lax.ppermute(
            lax.slice_in_dim(block, block.shape[dim] - width, None, axis=dim), axis, forward
        )
        high = lax.ppermute(lax.slice_in_dim(block, 0, width, axis=dim), axis, backward)
        block = jnp.concatenate([low, block, high], axis=dim)
    return block


def norm_mat(m):
    return m / jnp.sum(m, axis=(-2, -1), keepdims=True)


def norm_vec(v):
    return v / jnp.sum(v, axis=-1, keepdims=True)


def mat_mat(a, b):
    return jnp.einsum("...im,...ml->...il", a, b, precision=HIGH)


def bit_reverse(x, axis):
    bits = x.shape[axis].bit_length() - 1
    split = x.shape[:axis] + (2,) * bits + x.shape[axis + 1 :]
    perm = (
        list(range(axis))
        + [axis + bits - 1 - i for i in range(bits)]
        + list(range(axis + bits, len(split)))
    )
    return jnp.transpose(x.reshape(split), perm).reshape(x.shape)


def chain(mats):
    while len(mats) > 1:
        half = len(mats) // 2
        left = jnp.stack(mats[0 : 2 * half : 2])
        right = jnp.stack(mats[1 : 2 * half : 2])
        joined = norm_mat(mat_mat(left, right))
        mats = [joined[i] for i in range(half)] + mats[2 * half :]
    return mats[0]


def group_scan(mats, axis, whole=True):
    count = lax.axis_size(axis)
    mine = lax.axis_index(axis)
    eye = jnp.eye(mats.shape[-1], dtype=mats.dtype)
    everyone = lax.all_gather(mats, axis)
    earlier = [jnp.where(mine > j, everyone[j], eye) for j in range(count)]
    if not whole:
        return chain(earlier), None
    both = chain([jnp.stack([earlier[j], everyone[j]]) for j in range(count)])
    return both[0], both[1]


def exclusive_scan(mats, axes):
    parts = []
    for depth, axis in enumerate(reversed(axes)):
        before, mats = group_scan(mats, axis, depth < len(axes) - 1)
        parts.append(before)
    return chain(parts[::-1])


def on_device(
    features,
    wear,
    rec_start,
    rec_end,
    conv_first,
    conv_second,
    emit_weight,
    leave,
    jump,
    init_logits,
    type_prior,
):
    persons = features.shape[1]
    span = features.shape[2]
    kinds = jump.shape[0]
    states = jump.shape[-1]
    tm_index = lax.axis_index(TM)
    type_index = lax.axis_index("type")
    people_index = lax.axis_index("people")
    tm_count = 1
    for axis in TM:
        tm_count *= lax.axis_size(axis)
    total_epochs = span * tm_count
    extended = padded(features, ((TM, 2),), 5)
    first = jnp.zeros((persons, span + 8, conv_first.shape[2]), jnp.float32)
    for tap in range(3):
        first = first + jnp.einsum(
            "ipt,ic->ptc",
            extended[:, :, tap : tap + span + 8],
            conv_first[tap],
            preferred_element_type=jnp.float32,
        )
    wide_pos = tm_index * span - 4 + jnp.arange(span + 8, dtype=jnp.int32)
    inside = (wide_pos >= 0) & (wide_pos < total_epochs)
    first = jnp.where(inside[None, :, None], jax.nn.silu(first), 0.0).astype(jnp.bfloat16)
    second = jnp.zeros((persons, span, conv_second.shape[2]), jnp.float32)
    for tap in range(3):
        second = second + jnp.einsum(
            "ptc,cd->ptd",
            first[:, 4 * tap : 4 * tap + span],
            conv_second[tap],
            preferred_element_type=jnp.float32,
        )
    second = jax.nn.silu(second).astype(jnp.bfloat16)
    logits = jnp.einsum("ptc,cm->ptm", second, emit_weight, preferred_element_type=jnp.float32)
    probs = jnp.exp(jax.nn.log_softmax(logits.reshape(persons, span, kinds, states), axis=-1))
    positions = tm_index * span + jnp.arange(span, dtype=jnp.int32)
    observed = (
        (wear > 0)
        & (positions[None, :] >= rec_start[:, None])
        & (positions[None, :] < rec_end[:, None])
    )
    emis = jnp.where(observed[:, :, None, None], probs, jnp.float32(1.0))
    observed_f = observed.astype(jnp.float32)
    eye_small = jnp.eye(states, dtype=jnp.float32)
    trans = (1.0 - leave)[..., None] * eye_small + leave[..., None] * jax.nn.softmax(jump, axis=-1)
    start = jax.nn.softmax(init_logits, axis=-1)

    order = bit_reverse(jnp.transpose(emis, (2, 0, 1, 3)), 2)
    half = span // 2
    e_even = order[:, :, :half]
    e_odd = order[:, :, half:]
    quarter = span // 4
    cols = [order[:, :, m * quarter : (m + 1) * quarter, None, :] for m in range(4)]
    left = trans[:, None, None] * cols[0]
    pair = norm_mat(jnp.einsum("kpjim,kml->kpjil", left, trans, precision=HIGH) * cols[2])
    level = norm_mat(jnp.einsum("kpjim,kml->kpjil", pair, trans, precision=HIGH) * cols[1])
    level = norm_mat(jnp.einsum("kpjim,kml->kpjil", level, trans, precision=HIGH) * cols[3])
    levels = [None, pair, level]
    while levels[-1].shape[2] > 1:
        last = levels[-1]
        n = last.shape[2] // 2
        levels.append(norm_mat(mat_mat(last[:, :, :n], last[:, :, n:])))
    device_op = levels[-1][:, :, 0]

    before = exclusive_scan(device_op, TM)
    alpha_in = norm_vec(jnp.einsum("ki,kpij->kpj", start, before, precision=HIGHEST))

    entry = alpha_in[:, :, None]
    for depth in range(len(levels) - 1, 1, -1):
        n = entry.shape[2]
        sibling = levels[depth - 1][:, :, :n]
        moved = norm_vec(jnp.einsum("kpni,kpnil->kpnl", entry, sibling, precision=HIGH))
        entry = jnp.concatenate([entry, moved], axis=2)
    u = jnp.einsum("kpji,kil->kpjl", entry, trans, precision=HIGH) * e_even
    c_even = jnp.sum(u, axis=-1)
    a_even = u / c_even[..., None]
    v = jnp.einsum("kpji,kil->kpjl", a_even, trans, precision=HIGH) * e_odd
    c_odd = jnp.sum(v, axis=-1)
    a_odd = v / c_odd[..., None]
    alpha = bit_reverse(jnp.concatenate([a_even, a_odd], axis=2), 2)
    filtered = jnp.transpose(alpha, (1, 2, 0, 3))
    own_log = jnp.transpose(jnp.sum(jnp.log(c_even), axis=2) + jnp.sum(jnp.log(c_odd), axis=2))
    occupied = jnp.einsum("pt,ptks->pks", observed_f, filtered, precision=HIGHEST)
    count = jnp.sum(observed_f, axis=1)

    halves_n = lax.axis_size("type")
    people_n = lax.axis_size("people") * persons
    row = jnp.concatenate(
        [own_log, occupied.reshape(persons, kinds * states), count[:, None]], axis=1
    )
    person_hot = (
        people_index * persons + jnp.arange(persons)[:, None] == jnp.arange(people_n)[None, :]
    ).astype(jnp.float32)
    half_hot = (type_index == jnp.arange(halves_n)).astype(jnp.float32)
    table = person_hot[:, :, None, None] * half_hot[None, None, :, None] * row[:, None, None, :]
    table = jnp.sum(table, axis=0)
    for axis in TM[::-1] + (("people", "type"),):
        table = lax.psum(table, axis)

    full = table[:, :, :kinds].reshape(people_n, halves_n * kinds)
    rate_full = full / total_epochs
    post_full = jax.nn.softmax(type_prior[None, :] + 8.0 * rate_full, axis=-1)
    offset = type_index * kinds
    mine = people_index * persons
    rate_own = lax.dynamic_slice(rate_full, (mine, offset), (persons, kinds))
    post_own = lax.dynamic_slice(post_full, (mine, offset), (persons, kinds))
    post_type = lax.dynamic_slice(post_full, (jnp.int32(0), offset), (people_n, kinds))
    occ_all = jnp.take(table, type_index, axis=1)[:, kinds : kinds + kinds * states]
    occ_all = occ_all.reshape(people_n, kinds, states)
    cnt_all = jnp.take(table, type_index, axis=1)[:, kinds + kinds * states]
    numer = jnp.einsum("pk,pks->ks", post_type, occ_all, precision=HIGHEST)
    denom = jnp.einsum("pk,p->k", post_type, cnt_all, precision=HIGHEST)
    occupancy = numer / denom[:, None]
    return (rate_own, post_own, occupancy, filtered)


def solution(mesh):
    people, epochs, halves = mesh.devices.shape
    assert epochs == TM_SPLIT[0] * TM_SPLIT[1] * TM_SPLIT[2]
    fine = jax.sharding.Mesh(
        mesh.devices.reshape((people,) + TM_SPLIT + (halves,)), ("people",) + TM + ("type",)
    )
    return jax.shard_map(
        on_device,
        mesh=fine,
        in_specs=(
            P(None, "people", TM),
            P("people", TM),
            P("people"),
            P("people"),
            P(),
            P(),
            P(None, "type"),
            P("type", None),
            P("type", None, None),
            P("type", None),
            P(),
        ),
        out_specs=(
            P("people", "type"),
            P("people", "type"),
            P("type", None),
            P("people", TM, "type", None),
        ),
        check_vma=False,
    )
```

```python
import jax
import jax.numpy as jnp
from jax import lax
from jax.sharding import PartitionSpec as P

HIGHEST = lax.Precision.HIGHEST
HIGH = lax.Precision.HIGH
TM_SPLIT = (8, 4, 2)
TM = ("tz", "ty", "tc")


def padded(block, sides, width):
    for axis, dim in sides:
        count = 1
        for name in axis:
            count *= lax.axis_size(name)
        forward = [(i, i + 1) for i in range(count - 1)]
        backward = [(target, source) for source, target in forward]
        low = lax.ppermute(
            lax.slice_in_dim(block, block.shape[dim] - width, None, axis=dim), axis, forward
        )
        high = lax.ppermute(lax.slice_in_dim(block, 0, width, axis=dim), axis, backward)
        block = jnp.concatenate([low, block, high], axis=dim)
    return block


def norm_mat(m):
    return m / jnp.sum(m, axis=(-2, -1), keepdims=True)


def norm_vec(v):
    return v / jnp.sum(v, axis=-1, keepdims=True)


def mat_mat(a, b):
    return jnp.einsum("...im,...ml->...il", a, b, precision=HIGH)


def bit_reverse(x, axis):
    bits = x.shape[axis].bit_length() - 1
    split = x.shape[:axis] + (2,) * bits + x.shape[axis + 1 :]
    perm = (
        list(range(axis))
        + [axis + bits - 1 - i for i in range(bits)]
        + list(range(axis + bits, len(split)))
    )
    return jnp.transpose(x.reshape(split), perm).reshape(x.shape)


def chain(mats):
    while mats.shape[0] > 1:
        half = mats.shape[0] // 2
        paired = mats[: 2 * half].reshape((half, 2) + mats.shape[1:])
        joined = norm_mat(mat_mat(paired[:, 0], paired[:, 1]))
        mats = jnp.concatenate([joined, mats[2 * half :]], axis=0)
    return mats[0]


def group_scan(mats, axis, whole=True):
    count = lax.axis_size(axis)
    mine = lax.axis_index(axis)
    eye = jnp.eye(mats.shape[-1], dtype=mats.dtype)
    everyone = lax.all_gather(mats, axis)
    keep = (jnp.arange(count) < mine).reshape((count,) + (1,) * mats.ndim)
    earlier = jnp.where(keep, everyone, eye)
    if not whole:
        return chain(earlier), None
    both = chain(jnp.stack([earlier, everyone], axis=1))
    return both[0], both[1]


def exclusive_scan(mats, axes):
    parts = []
    for depth, axis in enumerate(reversed(axes)):
        before, mats = group_scan(mats, axis, depth < len(axes) - 1)
        parts.append(before)
    return chain(jnp.stack(parts[::-1]))


def on_device(
    features,
    wear,
    rec_start,
    rec_end,
    conv_first,
    conv_second,
    emit_weight,
    leave,
    jump,
    init_logits,
    type_prior,
):
    persons = features.shape[1]
    span = features.shape[2]
    kinds = jump.shape[0]
    states = jump.shape[-1]
    tm_index = lax.axis_index(TM)
    type_index = lax.axis_index("type")
    people_index = lax.axis_index("people")
    tm_count = 1
    for axis in TM:
        tm_count *= lax.axis_size(axis)
    total_epochs = span * tm_count
    extended = padded(features, ((TM, 2),), 5)
    taps_first = jnp.stack([extended[:, :, tap : tap + span + 8] for tap in range(3)])
    first = jnp.einsum(
        "jipt,jic->ptc", taps_first, conv_first, preferred_element_type=jnp.float32
    )
    wide_pos = tm_index * span - 4 + jnp.arange(span + 8, dtype=jnp.int32)
    inside = (wide_pos >= 0) & (wide_pos < total_epochs)
    first = jnp.where(inside[None, :, None], jax.nn.silu(first), 0.0).astype(jnp.bfloat16)
    taps_second = jnp.stack([first[:, 4 * tap : 4 * tap + span] for tap in range(3)])
    second = jnp.einsum(
        "jptc,jcd->ptd", taps_second, conv_second, preferred_element_type=jnp.float32
    )
    second = jax.nn.silu(second).astype(jnp.bfloat16)
    logits = jnp.einsum("ptc,cm->ptm", second, emit_weight, preferred_element_type=jnp.float32)
    probs = jnp.exp(jax.nn.log_softmax(logits.reshape(persons, span, kinds, states), axis=-1))
    positions = tm_index * span + jnp.arange(span, dtype=jnp.int32)
    observed = (
        (wear > 0)
        & (positions[None, :] >= rec_start[:, None])
        & (positions[None, :] < rec_end[:, None])
    )
    emis = jnp.where(observed[:, :, None, None], probs, jnp.float32(1.0))
    observed_f = observed.astype(jnp.float32)
    eye_small = jnp.eye(states, dtype=jnp.float32)
    trans = (1.0 - leave)[..., None] * eye_small + leave[..., None] * jax.nn.softmax(jump, axis=-1)
    start = jax.nn.softmax(init_logits, axis=-1)

    order = bit_reverse(jnp.transpose(emis, (2, 0, 1, 3)), 2)
    half = span // 2
    e_even = order[:, :, :half]
    e_odd = order[:, :, half:]
    quarter = span // 4
    cols = [order[:, :, m * quarter : (m + 1) * quarter, None, :] for m in range(4)]
    left = trans[:, None, None] * cols[0]
    pair = norm_mat(jnp.einsum("kpjim,kml->kpjil", left, trans, precision=HIGH) * cols[2])
    def extend(carry, col):
        grown = jnp.einsum("kpjim,kml->kpjil", carry, trans, precision=HIGH) * col
        return norm_mat(grown), None

    level, _ = lax.scan(extend, pair, jnp.stack([cols[1], cols[3]]))
    levels = [None, pair, level]
    while levels[-1].shape[2] > 1:
        last = levels[-1]
        n = last.shape[2] // 2
        levels.append(norm_mat(mat_mat(last[:, :, :n], last[:, :, n:])))
    device_op = levels[-1][:, :, 0]

    before = exclusive_scan(device_op, TM)
    alpha_in = norm_vec(jnp.einsum("ki,kpij->kpj", start, before, precision=HIGH))

    entry = alpha_in[:, :, None]
    for depth in range(len(levels) - 1, 1, -1):
        n = entry.shape[2]
        sibling = levels[depth - 1][:, :, :n]
        moved = norm_vec(jnp.einsum("kpni,kpnil->kpnl", entry, sibling, precision=HIGH))
        entry = jnp.concatenate([entry, moved], axis=2)
    u = jnp.einsum("kpji,kil->kpjl", entry, trans, precision=HIGH) * e_even
    c_even = jnp.sum(u, axis=-1)
    a_even = u / c_even[..., None]
    v = jnp.einsum("kpji,kil->kpjl", a_even, trans, precision=HIGH) * e_odd
    c_odd = jnp.sum(v, axis=-1)
    a_odd = v / c_odd[..., None]
    alpha = bit_reverse(jnp.concatenate([a_even, a_odd], axis=2), 2)
    filtered = jnp.transpose(alpha, (1, 2, 0, 3))
    own_log = jnp.transpose(jnp.sum(jnp.log(c_even), axis=2) + jnp.sum(jnp.log(c_odd), axis=2))
    occupied = jnp.einsum("pt,ptks->pks", observed_f, filtered, precision=HIGH)
    count = jnp.sum(observed_f, axis=1)

    halves_n = lax.axis_size("type")
    people_n = lax.axis_size("people") * persons
    row = jnp.concatenate(
        [own_log, occupied.reshape(persons, kinds * states), count[:, None]], axis=1
    )
    person_hot = (
        people_index * persons + jnp.arange(persons)[:, None] == jnp.arange(people_n)[None, :]
    ).astype(jnp.float32)
    half_hot = (type_index == jnp.arange(halves_n)).astype(jnp.float32)
    table = person_hot[:, :, None, None] * half_hot[None, None, :, None] * row[:, None, None, :]
    table = jnp.sum(table, axis=0)
    for axis in TM[::-1] + (("people", "type"),):
        table = lax.psum(table, axis)

    full = table[:, :, :kinds].reshape(people_n, halves_n * kinds)
    rate_full = full / total_epochs
    post_full = jax.nn.softmax(type_prior[None, :] + 8.0 * rate_full, axis=-1)
    offset = type_index * kinds
    mine = people_index * persons
    rate_own = lax.dynamic_slice(rate_full, (mine, offset), (persons, kinds))
    post_own = lax.dynamic_slice(post_full, (mine, offset), (persons, kinds))
    post_type = lax.dynamic_slice(post_full, (jnp.int32(0), offset), (people_n, kinds))
    occ_all = jnp.take(table, type_index, axis=1)[:, kinds : kinds + kinds * states]
    occ_all = occ_all.reshape(people_n, kinds, states)
    cnt_all = jnp.take(table, type_index, axis=1)[:, kinds + kinds * states]
    numer = jnp.einsum("pk,pks->ks", post_type, occ_all, precision=HIGHEST)
    denom = jnp.einsum("pk,p->k", post_type, cnt_all, precision=HIGHEST)
    occupancy = numer / denom[:, None]
    return (rate_own, post_own, occupancy, filtered)


def solution(mesh):
    people, epochs, halves = mesh.devices.shape
    assert epochs == TM_SPLIT[0] * TM_SPLIT[1] * TM_SPLIT[2]
    fine = jax.sharding.Mesh(
        mesh.devices.reshape((people,) + TM_SPLIT + (halves,)), ("people",) + TM + ("type",)
    )
    return jax.shard_map(
        on_device,
        mesh=fine,
        in_specs=(
            P(None, "people", TM),
            P("people", TM),
            P("people"),
            P("people"),
            P(),
            P(),
            P(None, "type"),
            P("type", None),
            P("type", None, None),
            P("type", None),
            P(),
        ),
        out_specs=(
            P("people", "type"),
            P("people", "type"),
            P("type", None),
            P("people", TM, "type", None),
        ),
        check_vma=False,
    )
```

```python
import jax
import jax.numpy as jnp
from jax import lax
from jax.sharding import PartitionSpec as P

HIGHEST = lax.Precision.HIGHEST
HIGH = lax.Precision.HIGH
TM_SPLIT = (8, 4, 2)
TM = ("tz", "ty", "tc")


def padded(block, sides, width):
    for axis, dim in sides:
        count = 1
        for name in axis:
            count *= lax.axis_size(name)
        forward = [(i, i + 1) for i in range(count - 1)]
        backward = [(target, source) for source, target in forward]
        low = lax.ppermute(
            lax.slice_in_dim(block, block.shape[dim] - width, None, axis=dim), axis, forward
        )
        high = lax.ppermute(lax.slice_in_dim(block, 0, width, axis=dim), axis, backward)
        block = jnp.concatenate([low, block, high], axis=dim)
    return block


def norm_mat(m):
    return m / jnp.sum(m, axis=(-2, -1), keepdims=True)


def norm_vec(v):
    return v / jnp.sum(v, axis=-1, keepdims=True)


def mat_mat(a, b):
    return jnp.einsum("...im,...ml->...il", a, b, precision=HIGH)


def bit_reverse(x, axis):
    bits = x.shape[axis].bit_length() - 1
    split = x.shape[:axis] + (2,) * bits + x.shape[axis + 1 :]
    perm = (
        list(range(axis))
        + [axis + bits - 1 - i for i in range(bits)]
        + list(range(axis + bits, len(split)))
    )
    return jnp.transpose(x.reshape(split), perm).reshape(x.shape)


def chain(mats):
    while mats.shape[0] > 1:
        half = mats.shape[0] // 2
        paired = mats[: 2 * half].reshape((half, 2) + mats.shape[1:])
        joined = norm_mat(mat_mat(paired[:, 0], paired[:, 1]))
        mats = jnp.concatenate([joined, mats[2 * half :]], axis=0)
    return mats[0]


def group_scan(mats, axis, whole=True):
    count = lax.axis_size(axis)
    mine = lax.axis_index(axis)
    eye = jnp.eye(mats.shape[-1], dtype=mats.dtype)
    everyone = lax.all_gather(mats, axis)
    keep = (jnp.arange(count) < mine).reshape((count,) + (1,) * mats.ndim)
    earlier = jnp.where(keep, everyone, eye)
    if not whole:
        return chain(earlier), None
    both = chain(jnp.stack([earlier, everyone], axis=1))
    return both[0], both[1]


def exclusive_scan(mats, axes):
    parts = []
    for depth, axis in enumerate(reversed(axes)):
        before, mats = group_scan(mats, axis, depth < len(axes) - 1)
        parts.append(before)
    return chain(jnp.stack(parts[::-1]))


def on_device(
    features,
    wear,
    rec_start,
    rec_end,
    conv_first,
    conv_second,
    emit_weight,
    leave,
    jump,
    init_logits,
    type_prior,
):
    persons = features.shape[1]
    span = features.shape[2]
    kinds = jump.shape[0]
    states = jump.shape[-1]
    tm_index = lax.axis_index(TM)
    type_index = lax.axis_index("type")
    people_index = lax.axis_index("people")
    tm_count = 1
    for axis in TM:
        tm_count *= lax.axis_size(axis)
    total_epochs = span * tm_count
    extended = padded(features, ((TM, 2),), 5)
    taps_first = jnp.stack([extended[:, :, tap : tap + span + 8] for tap in range(3)])
    first = jnp.einsum(
        "jipt,jic->ptc", taps_first, conv_first, preferred_element_type=jnp.float32
    )
    wide_pos = tm_index * span - 4 + jnp.arange(span + 8, dtype=jnp.int32)
    inside = (wide_pos >= 0) & (wide_pos < total_epochs)
    first = jnp.where(inside[None, :, None], jax.nn.silu(first), 0.0).astype(jnp.bfloat16)
    taps_second = jnp.stack([first[:, 4 * tap : 4 * tap + span] for tap in range(3)])
    second = jnp.einsum(
        "jptc,jcd->ptd", taps_second, conv_second, preferred_element_type=jnp.float32
    )
    second = jax.nn.silu(second).astype(jnp.bfloat16)
    logits = jnp.einsum("ptc,cm->ptm", second, emit_weight, preferred_element_type=jnp.float32)
    probs = jnp.exp(jax.nn.log_softmax(logits.reshape(persons, span, kinds, states), axis=-1))
    positions = tm_index * span + jnp.arange(span, dtype=jnp.int32)
    observed = (
        (wear > 0)
        & (positions[None, :] >= rec_start[:, None])
        & (positions[None, :] < rec_end[:, None])
    )
    emis = jnp.where(observed[:, :, None, None], probs, jnp.float32(1.0))
    observed_f = observed.astype(jnp.float32)
    eye_small = jnp.eye(states, dtype=jnp.float32)
    trans = (1.0 - leave)[..., None] * eye_small + leave[..., None] * jax.nn.softmax(jump, axis=-1)
    start = jax.nn.softmax(init_logits, axis=-1)

    order = bit_reverse(jnp.transpose(emis, (2, 0, 1, 3)), 2)
    half = span // 2
    e_even = order[:, :, :half]
    e_odd = order[:, :, half:]
    quarter = span // 4
    cols = [order[:, :, m * quarter : (m + 1) * quarter, None, :] for m in range(4)]
    left = trans[:, None, None] * cols[0]
    pair = norm_mat(jnp.einsum("kpjim,kml->kpjil", left, trans, precision=HIGH) * cols[2])
    level = norm_mat(jnp.einsum("kpjim,kml->kpjil", pair, trans, precision=HIGH) * cols[1])
    level = norm_mat(jnp.einsum("kpjim,kml->kpjil", level, trans, precision=HIGH) * cols[3])
    levels = [None, pair, level]
    while levels[-1].shape[2] > 1:
        last = levels[-1]
        n = last.shape[2] // 2
        levels.append(norm_mat(mat_mat(last[:, :, :n], last[:, :, n:])))
    device_op = levels[-1][:, :, 0]

    before = exclusive_scan(device_op, TM)
    alpha_in = norm_vec(jnp.einsum("ki,kpij->kpj", start, before, precision=HIGH))

    entry = alpha_in[:, :, None]
    for depth in range(len(levels) - 1, 1, -1):
        n = entry.shape[2]
        sibling = levels[depth - 1][:, :, :n]
        moved = norm_vec(jnp.einsum("kpni,kpnil->kpnl", entry, sibling, precision=HIGH))
        entry = jnp.concatenate([entry, moved], axis=2)
    u = jnp.einsum("kpji,kil->kpjl", entry, trans, precision=HIGH) * e_even
    c_even = jnp.sum(u, axis=-1)
    a_even = u / c_even[..., None]
    v = jnp.einsum("kpji,kil->kpjl", a_even, trans, precision=HIGH) * e_odd
    c_odd = jnp.sum(v, axis=-1)
    a_odd = v / c_odd[..., None]
    alpha = bit_reverse(jnp.concatenate([a_even, a_odd], axis=2), 2)
    filtered = jnp.transpose(alpha, (1, 2, 0, 3))
    own_log = jnp.transpose(jnp.sum(jnp.log(c_even), axis=2) + jnp.sum(jnp.log(c_odd), axis=2))
    occupied = jnp.einsum("pt,ptks->pks", observed_f, filtered, precision=HIGH)
    count = jnp.sum(observed_f, axis=1)

    halves_n = lax.axis_size("type")
    people_n = lax.axis_size("people") * persons
    row = jnp.concatenate(
        [own_log, occupied.reshape(persons, kinds * states), count[:, None]], axis=1
    )
    person_hot = (
        people_index * persons + jnp.arange(persons)[:, None] == jnp.arange(people_n)[None, :]
    ).astype(jnp.float32)
    half_hot = (type_index == jnp.arange(halves_n)).astype(jnp.float32)
    table = person_hot[:, :, None, None] * half_hot[None, None, :, None] * row[:, None, None, :]
    table = jnp.sum(table, axis=0)
    for axis in TM[::-1] + (("people", "type"),):
        table = lax.psum(table, axis)

    full = table[:, :, :kinds].reshape(people_n, halves_n * kinds)
    rate_full = full / total_epochs
    post_full = jax.nn.softmax(type_prior[None, :] + 8.0 * rate_full, axis=-1)
    offset = type_index * kinds
    mine = people_index * persons
    rate_own = lax.dynamic_slice(rate_full, (mine, offset), (persons, kinds))
    post_own = lax.dynamic_slice(post_full, (mine, offset), (persons, kinds))
    post_type = lax.dynamic_slice(post_full, (jnp.int32(0), offset), (people_n, kinds))
    occ_all = jnp.take(table, type_index, axis=1)[:, kinds : kinds + kinds * states]
    occ_all = occ_all.reshape(people_n, kinds, states)
    cnt_all = jnp.take(table, type_index, axis=1)[:, kinds + kinds * states]
    numer = jnp.einsum("pk,pks->ks", post_type, occ_all, precision=HIGH)
    denom = jnp.einsum("pk,p->k", post_type, cnt_all, precision=HIGH)
    occupancy = numer / denom[:, None]
    return (rate_own, post_own, occupancy, filtered)


def solution(mesh):
    people, epochs, halves = mesh.devices.shape
    assert epochs == TM_SPLIT[0] * TM_SPLIT[1] * TM_SPLIT[2]
    fine = jax.sharding.Mesh(
        mesh.devices.reshape((people,) + TM_SPLIT + (halves,)), ("people",) + TM + ("type",)
    )
    return jax.shard_map(
        on_device,
        mesh=fine,
        in_specs=(
            P(None, "people", TM),
            P("people", TM),
            P("people"),
            P("people"),
            P(),
            P(),
            P(None, "type"),
            P("type", None),
            P("type", None, None),
            P("type", None),
            P(),
        ),
        out_specs=(
            P("people", "type"),
            P("people", "type"),
            P("type", None),
            P("people", TM, "type", None),
        ),
        check_vma=False,
    )
```

```python
import jax
import jax.numpy as jnp
from jax import lax
from jax.sharding import PartitionSpec as P

HIGHEST = lax.Precision.HIGHEST
HIGH = lax.Precision.HIGH
TM_SPLIT = (8, 4, 2)
TM = ("tz", "ty", "tc")


def padded(block, sides, width):
    for axis, dim in sides:
        count = 1
        for name in axis:
            count *= lax.axis_size(name)
        forward = [(i, i + 1) for i in range(count - 1)]
        backward = [(target, source) for source, target in forward]
        low = lax.ppermute(
            lax.slice_in_dim(block, block.shape[dim] - width, None, axis=dim), axis, forward
        )
        high = lax.ppermute(lax.slice_in_dim(block, 0, width, axis=dim), axis, backward)
        block = jnp.concatenate([low, block, high], axis=dim)
    return block


def norm_mat(m):
    return m / jnp.sum(m, axis=(-2, -1), keepdims=True)


def norm_vec(v):
    return v / jnp.sum(v, axis=-1, keepdims=True)


def mat_mat(a, b):
    return jnp.einsum("...im,...ml->...il", a, b, precision=HIGH)


def bit_reverse(x, axis):
    bits = x.shape[axis].bit_length() - 1
    split = x.shape[:axis] + (2,) * bits + x.shape[axis + 1 :]
    perm = (
        list(range(axis))
        + [axis + bits - 1 - i for i in range(bits)]
        + list(range(axis + bits, len(split)))
    )
    return jnp.transpose(x.reshape(split), perm).reshape(x.shape)


def chain(mats):
    while mats.shape[0] > 1:
        half = mats.shape[0] // 2
        paired = mats[: 2 * half].reshape((half, 2) + mats.shape[1:])
        joined = norm_mat(mat_mat(paired[:, 0], paired[:, 1]))
        mats = jnp.concatenate([joined, mats[2 * half :]], axis=0)
    return mats[0]


def group_scan(mats, axis, whole=True):
    count = lax.axis_size(axis)
    mine = lax.axis_index(axis)
    eye = jnp.eye(mats.shape[-1], dtype=mats.dtype)
    everyone = lax.all_gather(mats.astype(jnp.bfloat16), axis).astype(mats.dtype)
    keep = (jnp.arange(count) < mine).reshape((count,) + (1,) * mats.ndim)
    earlier = jnp.where(keep, everyone, eye)
    if not whole:
        return chain(earlier), None
    both = chain(jnp.stack([earlier, everyone], axis=1))
    return both[0], both[1]


def exclusive_scan(mats, axes):
    parts = []
    for depth, axis in enumerate(reversed(axes)):
        before, mats = group_scan(mats, axis, depth < len(axes) - 1)
        parts.append(before)
    return chain(jnp.stack(parts[::-1]))


def on_device(
    features,
    wear,
    rec_start,
    rec_end,
    conv_first,
    conv_second,
    emit_weight,
    leave,
    jump,
    init_logits,
    type_prior,
):
    persons = features.shape[1]
    span = features.shape[2]
    kinds = jump.shape[0]
    states = jump.shape[-1]
    tm_index = lax.axis_index(TM)
    type_index = lax.axis_index("type")
    people_index = lax.axis_index("people")
    tm_count = 1
    for axis in TM:
        tm_count *= lax.axis_size(axis)
    total_epochs = span * tm_count
    extended = padded(features, ((TM, 2),), 5)
    taps_first = jnp.stack([extended[:, :, tap : tap + span + 8] for tap in range(3)])
    first = jnp.einsum(
        "jipt,jic->ptc", taps_first, conv_first, preferred_element_type=jnp.float32
    )
    wide_pos = tm_index * span - 4 + jnp.arange(span + 8, dtype=jnp.int32)
    inside = (wide_pos >= 0) & (wide_pos < total_epochs)
    first = jnp.where(inside[None, :, None], jax.nn.silu(first), 0.0).astype(jnp.bfloat16)
    taps_second = jnp.stack([first[:, 4 * tap : 4 * tap + span] for tap in range(3)])
    second = jnp.einsum(
        "jptc,jcd->ptd", taps_second, conv_second, preferred_element_type=jnp.float32
    )
    second = jax.nn.silu(second).astype(jnp.bfloat16)
    logits = jnp.einsum("ptc,cm->ptm", second, emit_weight, preferred_element_type=jnp.float32)
    probs = jnp.exp(jax.nn.log_softmax(logits.reshape(persons, span, kinds, states), axis=-1))
    positions = tm_index * span + jnp.arange(span, dtype=jnp.int32)
    observed = (
        (wear > 0)
        & (positions[None, :] >= rec_start[:, None])
        & (positions[None, :] < rec_end[:, None])
    )
    emis = jnp.where(observed[:, :, None, None], probs, jnp.float32(1.0))
    observed_f = observed.astype(jnp.float32)
    eye_small = jnp.eye(states, dtype=jnp.float32)
    trans = (1.0 - leave)[..., None] * eye_small + leave[..., None] * jax.nn.softmax(jump, axis=-1)
    start = jax.nn.softmax(init_logits, axis=-1)

    order = bit_reverse(jnp.transpose(emis, (2, 0, 1, 3)), 2)
    half = span // 2
    e_even = order[:, :, :half]
    e_odd = order[:, :, half:]
    quarter = span // 4
    cols = [order[:, :, m * quarter : (m + 1) * quarter, None, :] for m in range(4)]
    left = trans[:, None, None] * cols[0]
    pair = norm_mat(jnp.einsum("kpjim,kml->kpjil", left, trans, precision=HIGH) * cols[2])
    level = norm_mat(jnp.einsum("kpjim,kml->kpjil", pair, trans, precision=HIGH) * cols[1])
    level = norm_mat(jnp.einsum("kpjim,kml->kpjil", level, trans, precision=HIGH) * cols[3])
    levels = [None, pair, level]
    while levels[-1].shape[2] > 1:
        last = levels[-1]
        n = last.shape[2] // 2
        levels.append(norm_mat(mat_mat(last[:, :, :n], last[:, :, n:])))
    device_op = levels[-1][:, :, 0]

    before = exclusive_scan(device_op, TM)
    alpha_in = norm_vec(jnp.einsum("ki,kpij->kpj", start, before, precision=HIGH))

    entry = alpha_in[:, :, None]
    for depth in range(len(levels) - 1, 1, -1):
        n = entry.shape[2]
        sibling = levels[depth - 1][:, :, :n]
        moved = norm_vec(jnp.einsum("kpni,kpnil->kpnl", entry, sibling, precision=HIGH))
        entry = jnp.concatenate([entry, moved], axis=2)
    u = jnp.einsum("kpji,kil->kpjl", entry, trans, precision=HIGH) * e_even
    c_even = jnp.sum(u, axis=-1)
    a_even = u / c_even[..., None]
    v = jnp.einsum("kpji,kil->kpjl", a_even, trans, precision=HIGH) * e_odd
    c_odd = jnp.sum(v, axis=-1)
    a_odd = v / c_odd[..., None]
    alpha = bit_reverse(jnp.concatenate([a_even, a_odd], axis=2), 2)
    filtered = jnp.transpose(alpha, (1, 2, 0, 3))
    own_log = jnp.transpose(jnp.sum(jnp.log(c_even), axis=2) + jnp.sum(jnp.log(c_odd), axis=2))
    occupied = jnp.einsum("pt,ptks->pks", observed_f, filtered, precision=HIGH)
    count = jnp.sum(observed_f, axis=1)

    halves_n = lax.axis_size("type")
    people_n = lax.axis_size("people") * persons
    row = jnp.concatenate(
        [own_log, occupied.reshape(persons, kinds * states), count[:, None]], axis=1
    )
    person_hot = (
        people_index * persons + jnp.arange(persons)[:, None] == jnp.arange(people_n)[None, :]
    ).astype(jnp.float32)
    half_hot = (type_index == jnp.arange(halves_n)).astype(jnp.float32)
    table = person_hot[:, :, None, None] * half_hot[None, None, :, None] * row[:, None, None, :]
    table = jnp.sum(table, axis=0)
    for axis in TM[::-1] + (("people", "type"),):
        table = lax.psum(table, axis)

    full = table[:, :, :kinds].reshape(people_n, halves_n * kinds)
    rate_full = full / total_epochs
    post_full = jax.nn.softmax(type_prior[None, :] + 8.0 * rate_full, axis=-1)
    offset = type_index * kinds
    mine = people_index * persons
    rate_own = lax.dynamic_slice(rate_full, (mine, offset), (persons, kinds))
    post_own = lax.dynamic_slice(post_full, (mine, offset), (persons, kinds))
    post_type = lax.dynamic_slice(post_full, (jnp.int32(0), offset), (people_n, kinds))
    occ_all = jnp.take(table, type_index, axis=1)[:, kinds : kinds + kinds * states]
    occ_all = occ_all.reshape(people_n, kinds, states)
    cnt_all = jnp.take(table, type_index, axis=1)[:, kinds + kinds * states]
    numer = jnp.einsum("pk,pks->ks", post_type, occ_all, precision=HIGH)
    denom = jnp.einsum("pk,p->k", post_type, cnt_all, precision=HIGH)
    occupancy = numer / denom[:, None]
    return (rate_own, post_own, occupancy, filtered)


def solution(mesh):
    people, epochs, halves = mesh.devices.shape
    assert epochs == TM_SPLIT[0] * TM_SPLIT[1] * TM_SPLIT[2]
    fine = jax.sharding.Mesh(
        mesh.devices.reshape((people,) + TM_SPLIT + (halves,)), ("people",) + TM + ("type",)
    )
    return jax.shard_map(
        on_device,
        mesh=fine,
        in_specs=(
            P(None, "people", TM),
            P("people", TM),
            P("people"),
            P("people"),
            P(),
            P(),
            P(None, "type"),
            P("type", None),
            P("type", None, None),
            P("type", None),
            P(),
        ),
        out_specs=(
            P("people", "type"),
            P("people", "type"),
            P("type", None),
            P("people", TM, "type", None),
        ),
        check_vma=False,
    )
```

```python
import jax
import jax.numpy as jnp
from jax import lax
from jax.sharding import PartitionSpec as P

HIGHEST = lax.Precision.HIGHEST
HIGH = lax.Precision.HIGH
TM_SPLIT = (8, 4, 2)
TM = ("tz", "ty", "tc")


def padded(block, sides, width):
    for axis, dim in sides:
        count = 1
        for name in axis:
            count *= lax.axis_size(name)
        forward = [(i, i + 1) for i in range(count - 1)]
        backward = [(target, source) for source, target in forward]
        low = lax.ppermute(
            lax.slice_in_dim(block, block.shape[dim] - width, None, axis=dim), axis, forward
        )
        high = lax.ppermute(lax.slice_in_dim(block, 0, width, axis=dim), axis, backward)
        block = jnp.concatenate([low, block, high], axis=dim)
    return block


def norm_mat(m):
    return m / jnp.sum(m, axis=(-2, -1), keepdims=True)


def norm_vec(v):
    return v / jnp.sum(v, axis=-1, keepdims=True)


def mat_mat(a, b):
    return jnp.einsum("...im,...ml->...il", a, b, precision=HIGH)


def bit_reverse(x, axis):
    bits = x.shape[axis].bit_length() - 1
    split = x.shape[:axis] + (2,) * bits + x.shape[axis + 1 :]
    perm = (
        list(range(axis))
        + [axis + bits - 1 - i for i in range(bits)]
        + list(range(axis + bits, len(split)))
    )
    return jnp.transpose(x.reshape(split), perm).reshape(x.shape)


def chain(mats):
    while mats.shape[0] > 1:
        half = mats.shape[0] // 2
        paired = mats[: 2 * half].reshape((half, 2) + mats.shape[1:])
        joined = norm_mat(mat_mat(paired[:, 0], paired[:, 1]))
        mats = jnp.concatenate([joined, mats[2 * half :]], axis=0)
    return mats[0]


def group_scan(mats, axis, whole=True):
    count = lax.axis_size(axis)
    mine = lax.axis_index(axis)
    eye = jnp.eye(mats.shape[-1], dtype=mats.dtype)
    everyone = lax.all_gather(mats.astype(jnp.bfloat16), axis).astype(mats.dtype)
    keep = (jnp.arange(count) < mine).reshape((count,) + (1,) * mats.ndim)
    earlier = jnp.where(keep, everyone, eye)
    if not whole:
        return chain(earlier), None
    both = chain(jnp.stack([earlier, everyone], axis=1))
    return both[0], both[1]


def exclusive_scan(mats, axes):
    parts = []
    for depth, axis in enumerate(reversed(axes)):
        before, mats = group_scan(mats, axis, depth < len(axes) - 1)
        parts.append(before)
    return chain(jnp.stack(parts[::-1]))


def on_device(
    features,
    wear,
    rec_start,
    rec_end,
    conv_first,
    conv_second,
    emit_weight,
    leave,
    jump,
    init_logits,
    type_prior,
):
    persons = features.shape[1]
    span = features.shape[2]
    kinds = jump.shape[0]
    states = jump.shape[-1]
    tm_index = lax.axis_index(TM)
    type_index = lax.axis_index("type")
    people_index = lax.axis_index("people")
    tm_count = 1
    for axis in TM:
        tm_count *= lax.axis_size(axis)
    total_epochs = span * tm_count
    extended = padded(features, ((TM, 2),), 5)
    taps_first = jnp.stack([extended[:, :, tap : tap + span + 8] for tap in range(3)])
    first = jnp.einsum(
        "jipt,jic->ptc", taps_first, conv_first, preferred_element_type=jnp.float32
    )
    wide_pos = tm_index * span - 4 + jnp.arange(span + 8, dtype=jnp.int32)
    inside = (wide_pos >= 0) & (wide_pos < total_epochs)
    first = jnp.where(inside[None, :, None], jax.nn.silu(first), 0.0).astype(jnp.bfloat16)
    taps_second = jnp.stack([first[:, 4 * tap : 4 * tap + span] for tap in range(3)])
    second = jnp.einsum(
        "jptc,jcd->ptd", taps_second, conv_second, preferred_element_type=jnp.float32
    )
    second = jax.nn.silu(second).astype(jnp.bfloat16)
    logits = jnp.einsum("ptc,cm->ptm", second, emit_weight, preferred_element_type=jnp.float32)
    probs = jnp.exp(jax.nn.log_softmax(logits.reshape(persons, span, kinds, states), axis=-1))
    positions = tm_index * span + jnp.arange(span, dtype=jnp.int32)
    observed = (
        (wear > 0)
        & (positions[None, :] >= rec_start[:, None])
        & (positions[None, :] < rec_end[:, None])
    )
    emis = jnp.where(observed[:, :, None, None], probs, jnp.float32(1.0))
    observed_f = observed.astype(jnp.float32)
    eye_small = jnp.eye(states, dtype=jnp.float32)
    trans = (1.0 - leave)[..., None] * eye_small + leave[..., None] * jax.nn.softmax(jump, axis=-1)
    start = jax.nn.softmax(init_logits, axis=-1)

    order = bit_reverse(jnp.transpose(emis, (2, 0, 1, 3)), 2)
    half = span // 2
    e_even = order[:, :, :half]
    e_odd = order[:, :, half:]
    quarter = span // 4
    cols = [order[:, :, m * quarter : (m + 1) * quarter, None, :] for m in range(4)]
    left = trans[:, None, None] * cols[0]
    pair = norm_mat(jnp.einsum("kpjim,kml->kpjil", left, trans, precision=HIGH) * cols[2])
    level = norm_mat(jnp.einsum("kpjim,kml->kpjil", pair, trans, precision=HIGH) * cols[1])
    level = norm_mat(jnp.einsum("kpjim,kml->kpjil", level, trans, precision=HIGH) * cols[3])
    levels = [None, pair, level]
    while levels[-1].shape[2] > 1:
        last = levels[-1]
        n = last.shape[2] // 2
        levels.append(norm_mat(mat_mat(last[:, :, :n], last[:, :, n:])))
    device_op = levels[-1][:, :, 0]

    before = exclusive_scan(device_op, TM)
    alpha_in = norm_vec(jnp.einsum("ki,kpij->kpj", start, before, precision=HIGH))

    entry = alpha_in[:, :, None]
    for depth in range(len(levels) - 1, 1, -1):
        n = entry.shape[2]
        sibling = levels[depth - 1][:, :, :n]
        moved = norm_vec(jnp.sum(entry[..., :, None] * sibling, axis=-2))
        entry = jnp.concatenate([entry, moved], axis=2)
    u = jnp.einsum("kpji,kil->kpjl", entry, trans, precision=HIGH) * e_even
    c_even = jnp.sum(u, axis=-1)
    a_even = u / c_even[..., None]
    v = jnp.einsum("kpji,kil->kpjl", a_even, trans, precision=HIGH) * e_odd
    c_odd = jnp.sum(v, axis=-1)
    a_odd = v / c_odd[..., None]
    alpha = bit_reverse(jnp.concatenate([a_even, a_odd], axis=2), 2)
    filtered = jnp.transpose(alpha, (1, 2, 0, 3))
    own_log = jnp.transpose(jnp.sum(jnp.log(c_even), axis=2) + jnp.sum(jnp.log(c_odd), axis=2))
    occupied = jnp.sum(observed_f[:, :, None, None] * filtered, axis=1)
    count = jnp.sum(observed_f, axis=1)

    halves_n = lax.axis_size("type")
    people_n = lax.axis_size("people") * persons
    row = jnp.concatenate(
        [own_log, occupied.reshape(persons, kinds * states), count[:, None]], axis=1
    )
    person_hot = (
        people_index * persons + jnp.arange(persons)[:, None] == jnp.arange(people_n)[None, :]
    ).astype(jnp.float32)
    half_hot = (type_index == jnp.arange(halves_n)).astype(jnp.float32)
    table = person_hot[:, :, None, None] * half_hot[None, None, :, None] * row[:, None, None, :]
    table = jnp.sum(table, axis=0)
    for axis in TM[::-1] + (("people", "type"),):
        table = lax.psum(table, axis)

    full = table[:, :, :kinds].reshape(people_n, halves_n * kinds)
    rate_full = full / total_epochs
    post_full = jax.nn.softmax(type_prior[None, :] + 8.0 * rate_full, axis=-1)
    offset = type_index * kinds
    mine = people_index * persons
    rate_own = lax.dynamic_slice(rate_full, (mine, offset), (persons, kinds))
    post_own = lax.dynamic_slice(post_full, (mine, offset), (persons, kinds))
    post_type = lax.dynamic_slice(post_full, (jnp.int32(0), offset), (people_n, kinds))
    occ_all = jnp.take(table, type_index, axis=1)[:, kinds : kinds + kinds * states]
    occ_all = occ_all.reshape(people_n, kinds, states)
    cnt_all = jnp.take(table, type_index, axis=1)[:, kinds + kinds * states]
    numer = jnp.sum(post_type[:, :, None] * occ_all, axis=0)
    denom = jnp.sum(post_type * cnt_all[:, None], axis=0)
    occupancy = numer / denom[:, None]
    return (rate_own, post_own, occupancy, filtered)


def solution(mesh):
    people, epochs, halves = mesh.devices.shape
    assert epochs == TM_SPLIT[0] * TM_SPLIT[1] * TM_SPLIT[2]
    fine = jax.sharding.Mesh(
        mesh.devices.reshape((people,) + TM_SPLIT + (halves,)), ("people",) + TM + ("type",)
    )
    return jax.shard_map(
        on_device,
        mesh=fine,
        in_specs=(
            P(None, "people", TM),
            P("people", TM),
            P("people"),
            P("people"),
            P(),
            P(),
            P(None, "type"),
            P("type", None),
            P("type", None, None),
            P("type", None),
            P(),
        ),
        out_specs=(
            P("people", "type"),
            P("people", "type"),
            P("type", None),
            P("people", TM, "type", None),
        ),
        check_vma=False,
    )
```

```python
import jax
import jax.numpy as jnp
from jax import lax
from jax.sharding import PartitionSpec as P

HIGHEST = lax.Precision.HIGHEST
HIGH = lax.Precision.HIGH
TM_SPLIT = (8, 4, 2)
TM = ("tz", "ty", "tc")


def padded(block, sides, width):
    for axis, dim in sides:
        count = 1
        for name in axis:
            count *= lax.axis_size(name)
        forward = [(i, i + 1) for i in range(count - 1)]
        backward = [(target, source) for source, target in forward]
        low = lax.ppermute(
            lax.slice_in_dim(block, block.shape[dim] - width, None, axis=dim), axis, forward
        )
        high = lax.ppermute(lax.slice_in_dim(block, 0, width, axis=dim), axis, backward)
        block = jnp.concatenate([low, block, high], axis=dim)
    return block


def norm_mat(m):
    return m / jnp.sum(m, axis=(-2, -1), keepdims=True)


def norm_vec(v):
    return v / jnp.sum(v, axis=-1, keepdims=True)


def mat_mat(a, b):
    return jnp.einsum("...im,...ml->...il", a, b, precision=HIGH)


def bit_reverse(x, axis):
    bits = x.shape[axis].bit_length() - 1
    split = x.shape[:axis] + (2,) * bits + x.shape[axis + 1 :]
    perm = (
        list(range(axis))
        + [axis + bits - 1 - i for i in range(bits)]
        + list(range(axis + bits, len(split)))
    )
    return jnp.transpose(x.reshape(split), perm).reshape(x.shape)


def chain(mats):
    while mats.shape[0] > 1:
        half = mats.shape[0] // 2
        paired = mats[: 2 * half].reshape((half, 2) + mats.shape[1:])
        joined = norm_mat(mat_mat(paired[:, 0], paired[:, 1]))
        mats = jnp.concatenate([joined, mats[2 * half :]], axis=0)
    return mats[0]


def group_scan(mats, axis, whole=True):
    count = lax.axis_size(axis)
    mine = lax.axis_index(axis)
    eye = jnp.eye(mats.shape[-1], dtype=mats.dtype)
    everyone = lax.all_gather(mats.astype(jnp.bfloat16), axis).astype(mats.dtype)
    keep = (jnp.arange(count) < mine).reshape((count,) + (1,) * mats.ndim)
    earlier = jnp.where(keep, everyone, eye)
    if not whole:
        return chain(earlier), None
    both = chain(jnp.stack([earlier, everyone], axis=1))
    return both[0], both[1]


def exclusive_scan(mats, axes):
    parts = []
    for depth, axis in enumerate(reversed(axes)):
        before, mats = group_scan(mats, axis, depth < len(axes) - 1)
        parts.append(before)
    return chain(jnp.stack(parts[::-1]))


def on_device(
    features,
    wear,
    rec_start,
    rec_end,
    conv_first,
    conv_second,
    emit_weight,
    leave,
    jump,
    init_logits,
    type_prior,
):
    persons = features.shape[1]
    span = features.shape[2]
    kinds = jump.shape[0]
    states = jump.shape[-1]
    tm_index = lax.axis_index(TM)
    type_index = lax.axis_index("type")
    people_index = lax.axis_index("people")
    tm_count = 1
    for axis in TM:
        tm_count *= lax.axis_size(axis)
    total_epochs = span * tm_count
    extended = padded(features, ((TM, 2),), 5)
    taps_first = jnp.stack([extended[:, :, tap : tap + span + 8] for tap in range(3)])
    first = jnp.einsum(
        "jipt,jic->ptc", taps_first, conv_first, preferred_element_type=jnp.float32
    )
    wide_pos = tm_index * span - 4 + jnp.arange(span + 8, dtype=jnp.int32)
    inside = (wide_pos >= 0) & (wide_pos < total_epochs)
    first = jnp.where(inside[None, :, None], jax.nn.silu(first), 0.0).astype(jnp.bfloat16)
    taps_second = jnp.stack([first[:, 4 * tap : 4 * tap + span] for tap in range(3)])
    second = jnp.einsum(
        "jptc,jcd->ptd", taps_second, conv_second, preferred_element_type=jnp.float32
    )
    second = jax.nn.silu(second).astype(jnp.bfloat16)
    logits = jnp.einsum("ptc,cm->ptm", second, emit_weight, preferred_element_type=jnp.float32)
    probs = jnp.exp(jax.nn.log_softmax(logits.reshape(persons, span, kinds, states), axis=-1))
    positions = tm_index * span + jnp.arange(span, dtype=jnp.int32)
    observed = (
        (wear > 0)
        & (positions[None, :] >= rec_start[:, None])
        & (positions[None, :] < rec_end[:, None])
    )
    emis = jnp.where(observed[:, :, None, None], probs, jnp.float32(1.0))
    observed_f = observed.astype(jnp.float32)
    eye_small = jnp.eye(states, dtype=jnp.float32)
    trans = (1.0 - leave)[..., None] * eye_small + leave[..., None] * jax.nn.softmax(jump, axis=-1)
    start = jax.nn.softmax(init_logits, axis=-1)

    order = bit_reverse(jnp.transpose(emis, (2, 0, 1, 3)), 2)
    half = span // 2
    e_even = order[:, :, :half]
    e_odd = order[:, :, half:]
    quarter = span // 4
    cols = [order[:, :, m * quarter : (m + 1) * quarter, None, :] for m in range(4)]
    left = trans[:, None, None] * cols[0]
    pair = norm_mat(jnp.einsum("kpjim,kml->kpjil", left, trans, precision=HIGH) * cols[2])
    level = norm_mat(jnp.einsum("kpjim,kml->kpjil", pair, trans, precision=HIGH) * cols[1])
    level = norm_mat(jnp.einsum("kpjim,kml->kpjil", level, trans, precision=HIGH) * cols[3])
    levels = [None, pair, level]
    while levels[-1].shape[2] > 1:
        last = levels[-1]
        n = last.shape[2] // 2
        levels.append(norm_mat(mat_mat(last[:, :, :n], last[:, :, n:])))
    device_op = levels[-1][:, :, 0]

    before = exclusive_scan(device_op, TM)
    alpha_in = norm_vec(jnp.einsum("ki,kpij->kpj", start, before, precision=HIGH))

    entry = alpha_in[:, :, None]
    for depth in range(len(levels) - 1, 1, -1):
        n = entry.shape[2]
        sibling = levels[depth - 1][:, :, :n]
        moved = norm_vec(jnp.einsum("kpni,kpnil->kpnl", entry, sibling, precision=HIGH))
        entry = jnp.concatenate([entry, moved], axis=2)
    u = jnp.einsum("kpji,kil->kpjl", entry, trans, precision=HIGH) * e_even
    c_even = jnp.sum(u, axis=-1)
    a_even = u / c_even[..., None]
    v = jnp.einsum("kpji,kil->kpjl", a_even, trans, precision=HIGH) * e_odd
    c_odd = jnp.sum(v, axis=-1)
    a_odd = v / c_odd[..., None]
    alpha = bit_reverse(jnp.concatenate([a_even, a_odd], axis=2), 2)
    filtered = jnp.transpose(alpha, (1, 2, 0, 3))
    own_log = jnp.transpose(jnp.sum(jnp.log(c_even), axis=2) + jnp.sum(jnp.log(c_odd), axis=2))
    occupied = jnp.einsum("pt,ptks->pks", observed_f, filtered, precision=HIGH)
    count = jnp.sum(observed_f, axis=1)

    halves_n = lax.axis_size("type")
    people_n = lax.axis_size("people") * persons
    row = jnp.concatenate(
        [own_log, occupied.reshape(persons, kinds * states), count[:, None]], axis=1
    )
    person_hot = (
        people_index * persons + jnp.arange(persons)[:, None] == jnp.arange(people_n)[None, :]
    ).astype(jnp.float32)
    half_hot = (type_index == jnp.arange(halves_n)).astype(jnp.float32)
    for axis in TM[::-1]:
        row = lax.psum(row, axis)
    table = person_hot[:, :, None, None] * half_hot[None, None, :, None] * row[:, None, None, :]
    table = lax.psum(jnp.sum(table, axis=0), ("people", "type"))

    full = table[:, :, :kinds].reshape(people_n, halves_n * kinds)
    rate_full = full / total_epochs
    post_full = jax.nn.softmax(type_prior[None, :] + 8.0 * rate_full, axis=-1)
    offset = type_index * kinds
    mine = people_index * persons
    rate_own = lax.dynamic_slice(rate_full, (mine, offset), (persons, kinds))
    post_own = lax.dynamic_slice(post_full, (mine, offset), (persons, kinds))
    post_type = lax.dynamic_slice(post_full, (jnp.int32(0), offset), (people_n, kinds))
    occ_all = jnp.take(table, type_index, axis=1)[:, kinds : kinds + kinds * states]
    occ_all = occ_all.reshape(people_n, kinds, states)
    cnt_all = jnp.take(table, type_index, axis=1)[:, kinds + kinds * states]
    numer = jnp.einsum("pk,pks->ks", post_type, occ_all, precision=HIGH)
    denom = jnp.einsum("pk,p->k", post_type, cnt_all, precision=HIGH)
    occupancy = numer / denom[:, None]
    return (rate_own, post_own, occupancy, filtered)


def solution(mesh):
    people, epochs, halves = mesh.devices.shape
    assert epochs == TM_SPLIT[0] * TM_SPLIT[1] * TM_SPLIT[2]
    fine = jax.sharding.Mesh(
        mesh.devices.reshape((people,) + TM_SPLIT + (halves,)), ("people",) + TM + ("type",)
    )
    return jax.shard_map(
        on_device,
        mesh=fine,
        in_specs=(
            P(None, "people", TM),
            P("people", TM),
            P("people"),
            P("people"),
            P(),
            P(),
            P(None, "type"),
            P("type", None),
            P("type", None, None),
            P("type", None),
            P(),
        ),
        out_specs=(
            P("people", "type"),
            P("people", "type"),
            P("type", None),
            P("people", TM, "type", None),
        ),
        check_vma=False,
    )
```

```python
import jax
import jax.numpy as jnp
from jax import lax
from jax.sharding import PartitionSpec as P

HIGHEST = lax.Precision.HIGHEST
HIGH = lax.Precision.HIGH
TM_SPLIT = (8, 4, 2)
TM = ("tz", "ty", "tc")


def padded(block, sides, width):
    for axis, dim in sides:
        count = 1
        for name in axis:
            count *= lax.axis_size(name)
        forward = [(i, i + 1) for i in range(count - 1)]
        backward = [(target, source) for source, target in forward]
        low = lax.ppermute(
            lax.slice_in_dim(block, block.shape[dim] - width, None, axis=dim), axis, forward
        )
        high = lax.ppermute(lax.slice_in_dim(block, 0, width, axis=dim), axis, backward)
        block = jnp.concatenate([low, block, high], axis=dim)
    return block


def norm_mat(m):
    return m / jnp.sum(m, axis=(-2, -1), keepdims=True)


def norm_vec(v):
    return v / jnp.sum(v, axis=-1, keepdims=True)


def mat_mat(a, b):
    return jnp.einsum("...im,...ml->...il", a, b, precision=HIGH)


def bit_reverse(x, axis):
    bits = x.shape[axis].bit_length() - 1
    split = x.shape[:axis] + (2,) * bits + x.shape[axis + 1 :]
    perm = (
        list(range(axis))
        + [axis + bits - 1 - i for i in range(bits)]
        + list(range(axis + bits, len(split)))
    )
    return jnp.transpose(x.reshape(split), perm).reshape(x.shape)


def chain(mats):
    while mats.shape[0] > 1:
        half = mats.shape[0] // 2
        paired = mats[: 2 * half].reshape((half, 2) + mats.shape[1:])
        joined = norm_mat(mat_mat(paired[:, 0], paired[:, 1]))
        mats = jnp.concatenate([joined, mats[2 * half :]], axis=0)
    return mats[0]


def group_scan(mats, axis, whole=True):
    count = lax.axis_size(axis)
    mine = lax.axis_index(axis)
    eye = jnp.eye(mats.shape[-1], dtype=mats.dtype)
    everyone = lax.all_gather(mats.astype(jnp.bfloat16), axis).astype(mats.dtype)
    keep = (jnp.arange(count) < mine).reshape((count,) + (1,) * mats.ndim)
    earlier = jnp.where(keep, everyone, eye)
    if not whole:
        return chain(earlier), None
    both = chain(jnp.stack([earlier, everyone], axis=1))
    return both[0], both[1]


def exclusive_scan(mats, axes):
    parts = []
    for depth, axis in enumerate(reversed(axes)):
        before, mats = group_scan(mats, axis, depth < len(axes) - 1)
        parts.append(before)
    return chain(jnp.stack(parts[::-1]))


def on_device(
    features,
    wear,
    rec_start,
    rec_end,
    conv_first,
    conv_second,
    emit_weight,
    leave,
    jump,
    init_logits,
    type_prior,
):
    persons = features.shape[1]
    span = features.shape[2]
    kinds = jump.shape[0]
    states = jump.shape[-1]
    tm_index = lax.axis_index(TM)
    type_index = lax.axis_index("type")
    people_index = lax.axis_index("people")
    tm_count = 1
    for axis in TM:
        tm_count *= lax.axis_size(axis)
    total_epochs = span * tm_count
    extended = padded(features, ((TM, 2),), 5)
    taps_first = jnp.stack([extended[:, :, tap : tap + span + 8] for tap in range(3)])
    first = jnp.einsum(
        "jipt,jic->ptc", taps_first, conv_first, preferred_element_type=jnp.float32
    )
    wide_pos = tm_index * span - 4 + jnp.arange(span + 8, dtype=jnp.int32)
    inside = (wide_pos >= 0) & (wide_pos < total_epochs)
    first = jnp.where(inside[None, :, None], jax.nn.silu(first), 0.0).astype(jnp.bfloat16)
    taps_second = jnp.stack([first[:, 4 * tap : 4 * tap + span] for tap in range(3)])
    second = jnp.einsum(
        "jptc,jcd->ptd", taps_second, conv_second, preferred_element_type=jnp.float32
    )
    second = jax.nn.silu(second).astype(jnp.bfloat16)
    logits = jnp.einsum("ptc,cm->ptm", second, emit_weight, preferred_element_type=jnp.float32)
    probs = jnp.exp(jax.nn.log_softmax(logits.reshape(persons, span, kinds, states), axis=-1))
    positions = tm_index * span + jnp.arange(span, dtype=jnp.int32)
    observed = (
        (wear > 0)
        & (positions[None, :] >= rec_start[:, None])
        & (positions[None, :] < rec_end[:, None])
    )
    emis = jnp.where(observed[:, :, None, None], probs, jnp.float32(1.0))
    observed_f = observed.astype(jnp.float32)
    eye_small = jnp.eye(states, dtype=jnp.float32)
    trans = (1.0 - leave)[..., None] * eye_small + leave[..., None] * jax.nn.softmax(jump, axis=-1)
    start = jax.nn.softmax(init_logits, axis=-1)

    order = bit_reverse(jnp.transpose(emis, (2, 0, 1, 3)), 2)
    half = span // 2
    e_even = order[:, :, :half]
    e_odd = order[:, :, half:]
    quarter = span // 4
    cols = [order[:, :, m * quarter : (m + 1) * quarter, None, :] for m in range(4)]
    left = trans[:, None, None] * cols[0]
    pair = norm_mat(jnp.einsum("kpjim,kml->kpjil", left, trans, precision=HIGH) * cols[2])
    level = norm_mat(jnp.einsum("kpjim,kml->kpjil", pair, trans, precision=HIGH) * cols[1])
    level = norm_mat(jnp.einsum("kpjim,kml->kpjil", level, trans, precision=HIGH) * cols[3])
    levels = [None, pair, level]
    while levels[-1].shape[2] > 1:
        last = levels[-1]
        n = last.shape[2] // 2
        levels.append(norm_mat(mat_mat(last[:, :, :n], last[:, :, n:])))
    device_op = levels[-1][:, :, 0]

    before = exclusive_scan(device_op, TM)
    alpha_in = norm_vec(jnp.einsum("ki,kpij->kpj", start, before, precision=HIGH))

    entry = alpha_in[:, :, None]
    for depth in range(len(levels) - 1, 1, -1):
        n = entry.shape[2]
        sibling = levels[depth - 1][:, :, :n]
        moved = norm_vec(jnp.einsum("kpni,kpnil->kpnl", entry, sibling, precision=HIGH))
        entry = jnp.concatenate([entry, moved], axis=2)
    u = jnp.einsum("kpji,kil->kpjl", entry, trans, precision=HIGH) * e_even
    c_even = jnp.sum(u, axis=-1)
    a_even = u / c_even[..., None]
    v = jnp.einsum("kpji,kil->kpjl", a_even, trans, precision=HIGH) * e_odd
    c_odd = jnp.sum(v, axis=-1)
    a_odd = v / c_odd[..., None]
    alpha = bit_reverse(jnp.concatenate([a_even, a_odd], axis=2), 2)
    filtered = jnp.transpose(alpha, (1, 2, 0, 3))
    own_log = jnp.transpose(jnp.sum(jnp.log(c_even), axis=2) + jnp.sum(jnp.log(c_odd), axis=2))
    occupied = jnp.einsum("pt,ptks->pks", observed_f, filtered, precision=HIGH)
    count = jnp.sum(observed_f, axis=1)

    halves_n = lax.axis_size("type")
    people_n = lax.axis_size("people") * persons
    row = jnp.concatenate(
        [own_log, occupied.reshape(persons, kinds * states), count[:, None]], axis=1
    )
    person_hot = (
        people_index * persons + jnp.arange(persons)[:, None] == jnp.arange(people_n)[None, :]
    ).astype(jnp.float32)
    half_hot = (type_index == jnp.arange(halves_n)).astype(jnp.float32)
    for axis in TM[::-1]:
        row = lax.psum(row, axis)
    gathered = lax.all_gather(row, ("people", "type"))
    table = jnp.transpose(
        gathered.reshape((people_n // persons, halves_n) + row.shape), (0, 2, 1, 3)
    ).reshape(people_n, halves_n, row.shape[-1])

    full = table[:, :, :kinds].reshape(people_n, halves_n * kinds)
    rate_full = full / total_epochs
    post_full = jax.nn.softmax(type_prior[None, :] + 8.0 * rate_full, axis=-1)
    offset = type_index * kinds
    mine = people_index * persons
    rate_own = lax.dynamic_slice(rate_full, (mine, offset), (persons, kinds))
    post_own = lax.dynamic_slice(post_full, (mine, offset), (persons, kinds))
    post_type = lax.dynamic_slice(post_full, (jnp.int32(0), offset), (people_n, kinds))
    occ_all = jnp.take(table, type_index, axis=1)[:, kinds : kinds + kinds * states]
    occ_all = occ_all.reshape(people_n, kinds, states)
    cnt_all = jnp.take(table, type_index, axis=1)[:, kinds + kinds * states]
    numer = jnp.einsum("pk,pks->ks", post_type, occ_all, precision=HIGH)
    denom = jnp.einsum("pk,p->k", post_type, cnt_all, precision=HIGH)
    occupancy = numer / denom[:, None]
    return (rate_own, post_own, occupancy, filtered)


def solution(mesh):
    people, epochs, halves = mesh.devices.shape
    assert epochs == TM_SPLIT[0] * TM_SPLIT[1] * TM_SPLIT[2]
    fine = jax.sharding.Mesh(
        mesh.devices.reshape((people,) + TM_SPLIT + (halves,)), ("people",) + TM + ("type",)
    )
    return jax.shard_map(
        on_device,
        mesh=fine,
        in_specs=(
            P(None, "people", TM),
            P("people", TM),
            P("people"),
            P("people"),
            P(),
            P(),
            P(None, "type"),
            P("type", None),
            P("type", None, None),
            P("type", None),
            P(),
        ),
        out_specs=(
            P("people", "type"),
            P("people", "type"),
            P("type", None),
            P("people", TM, "type", None),
        ),
        check_vma=False,
    )
```
